1024 devices in a mesh: seq: 16 (over z, x_lo), head: 64 (over y, x_hi, core).
Axes of the slice: x: 8 (x_hi: 4, x_lo: 2; x = x_hi * 2 + x_lo), y: 8, z: 8, core: 2. Of those that a mesh axis runs over, the one named last changes fastest.
Arguments:
- queries: bfloat16 [4096, 8192], P('seq', 'head'), may hold values from -41 to 41
- keys: bfloat16 [16, 1600, 8, 128], P('seq', 'head'), may hold values from -4 to 4
- values: bfloat16 [16, 1600, 8, 128], P('seq', 'head'), may hold values from -6 to 6
- cotangent: bfloat16 [4096, 8192], P('seq', 'head'), may hold values from -6 to 6
- mask: int32 [4096, 2], P('seq'), may hold values from 0 to 1, as said below
Outputs:
- attended: bfloat16 [4096, 8192], P('seq', 'head')
- grad_query: bfloat16 [4096, 8192], P('seq', 'head')
- grad_keys: bfloat16 [16, 1600, 8, 128], P('seq', 'head')
- grad_values: bfloat16 [16, 1600, 8, 128], P('seq', 'head')
The draws below stay inside these ranges and needn't reach their ends.
Inputs may be any that keep to these rules, and one draw needn't show every extreme that they name: mask[t, 0] is 1 where token t attends to the image of its own block of 256 tokens, mask[t, 1] where it attends to the image of the block before. Within each block the ones of column 0 form a suffix that covers at least the block's second half, the ones of column 1 a prefix that holds the block's first token and at most its first 128 tokens, exactly that many in block 1; column 1 is all 0 on the first block.
All inputs are finite; a program needn't handle non-finite values.
Results may differ from the reference program's by a relative error of at most 0.038.
Values may be sent and summed in bfloat16 or wider, within the bound.
No kernel may reach another device: no remote copies, remote signals or barrier semaphores. Data moves between devices by JAX's collectives and lax.ppermute only.
A program may use at most 32 MiB of HBM per device.

```python
import jax
import jax.numpy as jnp
from jax import lax

QH = 64
KVH = 8
HD = 128
TXT = 256
VTOK = 1600
HPD = 1
IMAGES = 16
TOKENS = 4096
N_SEQ = 16
N_HEAD = 64


def key_field(key):
    field = jnp.clip(jax.random.normal(jax.random.fold_in(key, 5), (IMAGES, VTOK, KVH, HD), jnp.float32), -4.0, 4.0)
    return field


def draw_keys(key, part):
    raw_keys = key_field(key)
    return raw_keys.astype(jnp.bfloat16)


def draw_queries(key, part):
    field = jnp.clip(2.0 * jax.random.normal(jax.random.fold_in(key, 21), (TOKENS, QH, HD), jnp.float32), -8.0, 8.0)
    return field.reshape(TOKENS, QH * HD).astype(jnp.bfloat16)


def draw_mask(key, part):
    suffix_start = jax.random.randint(jax.random.fold_in(key, 11), (IMAGES,), 0, TXT // 2)
    prefix_end = jax.random.randint(jax.random.fold_in(key, 12), (IMAGES,), 1, TXT // 2 + 1)
    block_ids = jnp.arange(IMAGES, dtype=jnp.int32)
    prefix_end = jnp.where(block_ids == 1, TXT // 2, prefix_end)
    prefix_end = jnp.where(block_ids == 0, 0, prefix_end)
    position = jnp.arange(TXT, dtype=jnp.int32)
    own_cols = (position[None, :] >= suffix_start[:, None]).astype(jnp.int32)
    prev_cols = (position[None, :] < prefix_end[:, None]).astype(jnp.int32)
    return jnp.stack([own_cols, prev_cols], axis=-1).reshape(TOKENS, 2)


def block_scale(rng, dims, cuts, smallest, top_value):
    loudness = 1.0
    for dim, shards_of in cuts:
        heights = jax.random.uniform(jax.random.fold_in(jax.random.fold_in(rng, 6), dim), (shards_of,), jnp.float32, smallest / len(cuts), top_value / len(cuts))
        loudness = loudness * jnp.repeat(jnp.exp(heights), dims[dim] // shards_of).reshape((-1,) + (1,) * (len(dims) - 1 - dim))
    return loudness


def scatter_about(stream_key, dims, width, most, shards=(), held_as=jnp.bfloat16):
    entries = jax.random.normal(stream_key, dims, jnp.float32) * width
    if len(shards) > 0:
        entries = block_scale(stream_key, dims, shards, -0.22, 0.18) * entries
    return jnp.clip(entries, min=-most, max=most).astype(held_as)


def setup_inputs(seed: int = 0) -> dict:
    splits = jax.random.split(jax.random.key(seed), 6)
    return {
        "queries": draw_queries(jax.random.fold_in(splits[5], 71), 0),
        "keys": draw_keys(jax.random.fold_in(splits[5], 71), 0),
        "values": scatter_about(splits[2], (IMAGES, VTOK, KVH, HD), 1.0, 6.0, ((0, 16), (1, 64))),
        "cotangent": scatter_about(splits[3], (TOKENS, QH * HD), 1.0, 6.0, ((0, 16), (1, 64))),
        "mask": draw_mask(jax.random.fold_in(splits[5], 71), 0),
    }


NEGATIVE = -1e30


def bround(array):
    return lax.optimization_barrier(array.astype(jnp.bfloat16)).astype(jnp.float32)


def expand_heads(kv_block):
    return jnp.repeat(kv_block.astype(jnp.float32), QH // KVH, axis=1)


def block_forward(query_block, key_block, value_block, keep_mask):
    key_wide = expand_heads(key_block)
    value_wide = expand_heads(value_block)
    scores = jnp.einsum("thd,khd->thk", query_block, key_wide) * (HD ** -0.5)
    scores = jnp.where(keep_mask[:, None, None] > 0, scores, NEGATIVE)
    highest = jnp.max(scores, axis=2)
    powered = jnp.exp(scores - highest[:, :, None])
    totals = jnp.sum(powered, axis=2)
    partial_value = jnp.einsum("thk,khd->thd", bround(powered), value_wide)
    return scores, highest, totals, partial_value, key_wide, value_wide


def fold_heads(term):
    blocks = term.reshape(VTOK, N_HEAD, HPD, HD).sum(axis=2)
    rounded = bround(blocks)
    return rounded.reshape(VTOK, KVH, N_HEAD // KVH, HD).sum(axis=2)


def block_backward(scores, highest, totals, live_rows, grad_block, row_delta, query_block, key_wide, value_wide):
    weights = live_rows[:, :, None] * jnp.exp(scores - highest[:, :, None]) / totals[:, :, None]
    grad_weights = jnp.einsum("thd,khd->thk", grad_block, value_wide)
    grad_scores = bround(weights * (grad_weights - row_delta[:, :, None]) * (HD ** -0.5))
    grad_query = jnp.einsum("thk,khd->thd", grad_scores, key_wide)
    key_part = jnp.einsum("thk,thd->khd", grad_scores, query_block)
    value_part = jnp.einsum("thk,thd->khd", bround(weights), grad_block)
    return grad_query, fold_heads(key_part), fold_heads(value_part)


def reference(queries, keys, values, cotangent, mask):
    query_blocks = queries.reshape(N_SEQ, TXT, QH, HD)
    grad_blocks = cotangent.reshape(N_SEQ, TXT, QH, HD)
    mask_blocks = mask.reshape(N_SEQ, TXT, 2)
    prev_keys = jnp.roll(keys, 1, axis=0)
    prev_values = jnp.roll(values, 1, axis=0)

    def one_block(inputs):
        query_raw, grad_raw, mask_block, key_own, value_own, key_prev, value_prev = inputs
        query_block = query_raw.astype(jnp.float32)
        grad_block = grad_raw.astype(jnp.float32)
        score_own, peak_own, total_own, partial_own, keyw_own, valw_own = block_forward(query_block, key_own, value_own, mask_block[:, 0])
        score_prev, peak_prev, total_prev, partial_prev, keyw_prev, valw_prev = block_forward(query_block, key_prev, value_prev, mask_block[:, 1])
        highest = jnp.maximum(peak_own, peak_prev)
        scale_own = jnp.exp(peak_own - highest)
        scale_prev = jnp.exp(peak_prev - highest)
        totals = scale_own * total_own + scale_prev * total_prev
        live_rows = ((mask_block[:, 0] + mask_block[:, 1]) > 0).astype(jnp.float32)[:, None]
        attended = (live_rows[:, :, None] * (scale_own[:, :, None] * partial_own + scale_prev[:, :, None] * partial_prev) / totals[:, :, None]).astype(jnp.bfloat16)
        row_delta = jnp.sum(grad_block * attended.astype(jnp.float32), axis=2)
        gq_own, gk_own, gv_own = block_backward(score_own, highest, totals, live_rows, grad_block, row_delta, query_block, keyw_own, valw_own)
        gq_prev, gk_prev, gv_prev = block_backward(score_prev, highest, totals, live_rows, grad_block, row_delta, query_block, keyw_prev, valw_prev)
        grad_query = (gq_own + gq_prev).astype(jnp.bfloat16)
        return attended, grad_query, gk_own, gv_own, gk_prev, gv_prev

    outputs = lax.map(one_block, (query_blocks, grad_blocks, mask_blocks, keys, values, prev_keys, prev_values))
    attended = outputs[0].reshape(TOKENS, QH * HD)
    grad_query = outputs[1].reshape(TOKENS, QH * HD)
    padding = jnp.zeros((1, VTOK, KVH, HD), jnp.float32)
    key_next = jnp.concatenate([outputs[4][1:], padding], axis=0)
    value_next = jnp.concatenate([outputs[5][1:], padding], axis=0)
    grad_keys = (outputs[2] + key_next).astype(jnp.bfloat16)
    grad_values = (outputs[3] + value_next).astype(jnp.bfloat16)
    return attended, grad_query, grad_keys, grad_values
```

```python
import jax
import jax.numpy as jnp
from jax import lax
from jax.sharding import Mesh
from jax.sharding import PartitionSpec as P

HD = 128

NEGATIVE = -1e30


def passed_along(value, axis, by):
    length = lax.axis_size(axis)
    pairs = [(i, i + by) for i in range(length) if 0 <= i + by < length]
    return lax.ppermute(value, axis, pairs)


def block_forward(query_rows, key_rows, value_rows, keep_mask):
    scores = jnp.einsum(
        "rd,kd->rk", query_rows, key_rows, preferred_element_type=jnp.float32
    ) * HD ** (-0.5)
    scores = jnp.where(keep_mask[:, None] > 0, scores, NEGATIVE)
    highest = jnp.max(scores, axis=1)
    powered = jnp.exp(scores - highest[:, None])
    totals = jnp.sum(powered, axis=1)
    partial_value = jnp.dot(
        powered.astype(jnp.bfloat16), value_rows, preferred_element_type=jnp.float32
    )
    return (scores, highest, totals, partial_value)


def block_backward(
    scores, highest, totals, live_rows, grad_rows, row_delta, query_rows, key_rows, value_rows
):
    weights = live_rows[:, None] * jnp.exp(scores - highest[:, None]) / totals[:, None]
    grad_weights = jnp.einsum(
        "rd,kd->rk", grad_rows, value_rows, preferred_element_type=jnp.float32
    )
    grad_scores = (weights * (grad_weights - row_delta[:, None]) * HD ** (-0.5)).astype(
        jnp.bfloat16
    )
    query_grad = jnp.dot(grad_scores, key_rows, preferred_element_type=jnp.float32)
    key_part = jnp.einsum(
        "rk,rd->kd", grad_scores, query_rows, preferred_element_type=jnp.float32
    ).astype(jnp.bfloat16)
    value_part = jnp.einsum(
        "rk,rd->kd", weights.astype(jnp.bfloat16), grad_rows, preferred_element_type=jnp.float32
    ).astype(jnp.bfloat16)
    return (query_grad, key_part, value_part)


def per_device(queries, keys, values, cotangent, mask):
    groups = lax.axis_size("y")
    copies = lax.axis_size("r")
    rows = keys.shape[1]
    own_kv = jnp.stack([keys[0], values[0]])
    prev_kv = passed_along(own_kv, "seq", 1)
    both = jnp.concatenate([own_kv, prev_kv])
    both = jnp.transpose(both, (2, 0, 1, 3))
    by_group = lax.all_to_all(both, "y", split_axis=0, concat_axis=0, tiled=True)
    gathered = lax.all_gather(by_group, "r", axis=0, tiled=True)
    key_own, value_own, key_prev, value_prev = (
        gathered[:, i].reshape(copies * groups * rows, HD) for i in range(4)
    )

    head_count = queries.shape[1] // HD
    keep_own = jnp.repeat(mask[:, 0], head_count)
    keep_prev = jnp.repeat(mask[:, 1], head_count)
    live_rows = (keep_own + keep_prev > 0).astype(jnp.float32)
    score_own, peak_own, total_own, partial_own = block_forward(
        queries, key_own, value_own, keep_own
    )
    score_prev, peak_prev, total_prev, partial_prev = block_forward(
        queries, key_prev, value_prev, keep_prev
    )
    highest = jnp.maximum(peak_own, peak_prev)
    scale_own = jnp.exp(peak_own - highest)
    scale_prev = jnp.exp(peak_prev - highest)
    totals = scale_own * total_own + scale_prev * total_prev
    attended = (
        live_rows[:, None]
        * (scale_own[:, None] * partial_own + scale_prev[:, None] * partial_prev)
        / totals[:, None]
    ).astype(jnp.bfloat16)
    row_delta = jnp.sum(cotangent.astype(jnp.float32) * attended.astype(jnp.float32), axis=1)
    gq_own, gk_own, gv_own = block_backward(
        score_own, highest, totals, live_rows, cotangent, row_delta, queries, key_own, value_own
    )
    gq_prev, gk_prev, gv_prev = block_backward(
        score_prev, highest, totals, live_rows, cotangent, row_delta, queries, key_prev, value_prev
    )
    grad_query = (gq_own + gq_prev).astype(jnp.bfloat16)

    parts = jnp.stack(
        [p.reshape(copies * groups, rows, HD) for p in (gk_own, gv_own, gk_prev, gv_prev)],
        axis=1,
    )
    summed = lax.psum_scatter(parts.reshape(copies * groups, -1), "r", scatter_dimension=0, tiled=True).reshape(groups, 4, rows, HD)
    returned = lax.all_to_all(summed, "y", split_axis=0, concat_axis=0, tiled=True)
    second = passed_along(returned[:, 2:], "seq", -1)
    total = returned[:, :2].astype(jnp.float32) + second.astype(jnp.float32)
    total = jnp.transpose(total, (1, 2, 0, 3)).astype(jnp.bfloat16)
    return (attended, grad_query, total[0][None], total[1][None])


def solution(mesh):
    seq_devices, head_devices = mesh.devices.shape
    groups = 8
    split = Mesh(
        mesh.devices.reshape(seq_devices, groups, head_devices // groups), ("seq", "y", "r")
    )
    heads = ("y", "r")
    return jax.shard_map(
        per_device,
        mesh=split,
        in_specs=(
            P("seq", heads),
            P("seq", heads, None, None),
            P("seq", heads, None, None),
            P("seq", heads),
            P("seq", None),
        ),
        out_specs=(
            P("seq", heads),
            P("seq", heads),
            P("seq", heads, None, None),
            P("seq", heads, None, None),
        ),
        check_vma=False,
    )
```

```python
import jax
import jax.numpy as jnp
from jax import lax
from jax.sharding import Mesh
from jax.sharding import PartitionSpec as P

HD = 128
KVH = 8

NEGATIVE = -1e30


def passed_along(value, axis, by):
    length = lax.axis_size(axis)
    pairs = [(i, i + by) for i in range(length) if 0 <= i + by < length]
    return lax.ppermute(value, axis, pairs)


def swapped(value):
    n = lax.axis_size("r")
    pairs = [(a * n + b, b * n + a) for a in range(n) for b in range(n)]
    return lax.ppermute(value, ("y", "r"), pairs)


def block_forward(query_rows, key_rows, value_rows, keep_mask):
    scores = jnp.einsum(
        "rd,kd->rk", query_rows, key_rows, preferred_element_type=jnp.float32
    ) * HD ** (-0.5)
    scores = jnp.where(keep_mask[:, None] > 0, scores, NEGATIVE)
    highest = jnp.max(scores, axis=1)
    powered = jnp.exp(scores - highest[:, None])
    totals = jnp.sum(powered, axis=1)
    partial_value = jnp.dot(
        powered.astype(jnp.bfloat16), value_rows, preferred_element_type=jnp.float32
    )
    return (scores, highest, totals, partial_value)


def block_backward(
    scores, highest, totals, live_rows, grad_rows, row_delta, query_rows, key_rows, value_rows
):
    weights = live_rows[:, None] * jnp.exp(scores - highest[:, None]) / totals[:, None]
    grad_weights = jnp.einsum(
        "rd,kd->rk", grad_rows, value_rows, preferred_element_type=jnp.float32
    )
    grad_scores = (weights * (grad_weights - row_delta[:, None]) * HD ** (-0.5)).astype(
        jnp.bfloat16
    )
    query_grad = jnp.dot(grad_scores, key_rows, preferred_element_type=jnp.float32)
    key_part = jnp.einsum(
        "rk,rd->kd", grad_scores, query_rows, preferred_element_type=jnp.float32
    ).astype(jnp.bfloat16)
    value_part = jnp.einsum(
        "rk,rd->kd", weights.astype(jnp.bfloat16), grad_rows, preferred_element_type=jnp.float32
    ).astype(jnp.bfloat16)
    return (query_grad, key_part, value_part)


def per_device(queries, keys, values, cotangent, mask):
    groups = lax.axis_size("y")
    copies = lax.axis_size("r")
    blocks = groups * copies
    rows = keys.shape[1]
    inputs = swapped(jnp.stack([queries, cotangent]))
    queries, cotangent = inputs[0], inputs[1]

    own_kv = jnp.stack([keys[0], values[0]])
    prev_kv = passed_along(own_kv, "seq", 1)
    both = jnp.transpose(jnp.concatenate([own_kv, prev_kv]), (0, 2, 1, 3))
    by_copy = lax.all_to_all(both, "r", split_axis=1, concat_axis=1, tiled=True)
    by_copy = by_copy.reshape(4, copies, rows * HD)
    gathered = lax.all_gather(by_copy, "y", axis=1, tiled=True)
    gathered = jnp.transpose(gathered.reshape(4, blocks, rows, HD), (0, 2, 1, 3))
    gathered = gathered.reshape(4, rows * blocks, HD)
    key_own, value_own, key_prev, value_prev = (gathered[i] for i in range(4))

    head_count = queries.shape[1] // HD
    keep_own = jnp.repeat(mask[:, 0], head_count)
    keep_prev = jnp.repeat(mask[:, 1], head_count)
    live_rows = (keep_own + keep_prev > 0).astype(jnp.float32)
    score_own, peak_own, total_own, partial_own = block_forward(
        queries, key_own, value_own, keep_own
    )
    score_prev, peak_prev, total_prev, partial_prev = block_forward(
        queries, key_prev, value_prev, keep_prev
    )
    highest = jnp.maximum(peak_own, peak_prev)
    scale_own = jnp.exp(peak_own - highest)
    scale_prev = jnp.exp(peak_prev - highest)
    totals = scale_own * total_own + scale_prev * total_prev
    attended = (
        live_rows[:, None]
        * (scale_own[:, None] * partial_own + scale_prev[:, None] * partial_prev)
        / totals[:, None]
    ).astype(jnp.bfloat16)
    row_delta = jnp.sum(cotangent.astype(jnp.float32) * attended.astype(jnp.float32), axis=1)
    gq_own, gk_own, gv_own = block_backward(
        score_own, highest, totals, live_rows, cotangent, row_delta, queries, key_own, value_own
    )
    gq_prev, gk_prev, gv_prev = block_backward(
        score_prev, highest, totals, live_rows, cotangent, row_delta, queries, key_prev, value_prev
    )
    grad_query = (gq_own + gq_prev).astype(jnp.bfloat16)
    outputs = swapped(jnp.stack([attended, grad_query]))

    parts = jnp.stack([gk_own, gv_own, gk_prev, gv_prev]).reshape(4, rows, blocks, HD)
    parts = jnp.transpose(parts, (2, 0, 1, 3)).reshape(blocks, -1)
    summed = lax.psum_scatter(parts, "y", scatter_dimension=0, tiled=True)
    summed = summed.reshape(copies, 4, rows, HD)
    returned = lax.all_to_all(summed, "r", split_axis=0, concat_axis=0, tiled=True)
    second = passed_along(returned[:, 2:], "seq", -1)
    total = returned[:, :2].astype(jnp.float32) + second.astype(jnp.float32)
    total = jnp.transpose(total, (1, 2, 0, 3)).astype(jnp.bfloat16)
    return (outputs[0], outputs[1], total[0][None], total[1][None])


def solution(mesh):
    seq_devices, head_devices = mesh.devices.shape
    split = Mesh(
        mesh.devices.reshape(seq_devices, KVH, head_devices // KVH), ("seq", "y", "r")
    )
    heads = ("y", "r")
    return jax.shard_map(
        per_device,
        mesh=split,
        in_specs=(
            P("seq", heads),
            P("seq", heads, None, None),
            P("seq", heads, None, None),
            P("seq", heads),
            P("seq", None),
        ),
        out_specs=(
            P("seq", heads),
            P("seq", heads),
            P("seq", heads, None, None),
            P("seq", heads, None, None),
        ),
        check_vma=False,
    )
```

```python
import jax
import jax.numpy as jnp
from jax import lax
from jax.sharding import Mesh
from jax.sharding import PartitionSpec as P

HD = 128
KVH = 8

NEGATIVE = -1e30


def passed_along(value, axis, by):
    length = lax.axis_size(axis)
    pairs = [(i, i + by) for i in range(length) if 0 <= i + by < length]
    return lax.ppermute(value, axis, pairs)


def block_forward(query_rows, key_rows, value_rows, keep_mask):
    scores = jnp.einsum(
        "rd,kd->rk", query_rows, key_rows, preferred_element_type=jnp.float32
    ) * HD ** (-0.5)
    scores = jnp.where(keep_mask[:, None] > 0, scores, NEGATIVE)
    highest = jnp.max(scores, axis=1)
    powered = jnp.exp(scores - highest[:, None])
    totals = jnp.sum(powered, axis=1)
    partial_value = jnp.dot(
        powered.astype(jnp.bfloat16), value_rows, preferred_element_type=jnp.float32
    )
    return (scores, highest, totals, partial_value)


def finish_backward(weights, grad_rows, row_delta, query_rows, key_rows, value_rows):
    grad_weights = jnp.einsum(
        "rd,kd->rk", grad_rows, value_rows, preferred_element_type=jnp.float32
    )
    grad_scores = (weights * (grad_weights - row_delta[:, None]) * HD ** (-0.5)).astype(
        jnp.bfloat16
    )
    query_grad = jnp.dot(grad_scores, key_rows, preferred_element_type=jnp.float32)
    key_part = jnp.einsum(
        "rk,rd->kd", grad_scores, query_rows, preferred_element_type=jnp.float32
    ).astype(jnp.bfloat16)
    value_part = jnp.einsum(
        "rk,rd->kd", weights.astype(jnp.bfloat16), grad_rows, preferred_element_type=jnp.float32
    ).astype(jnp.bfloat16)
    return (query_grad, key_part, value_part)


def per_device(queries, keys, values, cotangent, mask):
    groups = lax.axis_size("y")
    copies = lax.axis_size("r")
    blocks = groups * copies
    rows = keys.shape[1]
    tokens = queries.shape[0]
    half = tokens // 2

    served = passed_along(jnp.stack([queries[:half], cotangent[:half]]), "seq", -1)
    query_next, grad_next = served[0], served[1]

    own_kv = jnp.stack([keys[0], values[0]])
    own_kv = jnp.transpose(own_kv, (0, 2, 1, 3)).reshape(2, KVH, rows * HD)
    by_group = lax.all_to_all(own_kv, "y", split_axis=1, concat_axis=1, tiled=True)
    gathered = lax.all_gather(by_group, "r", axis=1, tiled=True)
    gathered = jnp.transpose(gathered.reshape(2, blocks, rows, HD), (0, 2, 1, 3))
    gathered = gathered.reshape(2, rows * blocks, HD)
    key_own, value_own = gathered[0], gathered[1]

    keep_own = mask[:, 0]
    keep_prev = mask[:, 1]
    live_rows = (keep_own + keep_prev > 0).astype(jnp.float32)
    score_own, peak_own, total_own, partial_own = block_forward(
        queries, key_own, value_own, keep_own
    )

    score_next = jnp.einsum(
        "rd,kd->rk", query_next, key_own, preferred_element_type=jnp.float32
    ) * HD ** (-0.5)
    peak_next = jnp.max(score_next, axis=1)
    total_next = jnp.sum(jnp.exp(score_next - peak_next[:, None]), axis=1)
    partial_next = jnp.dot(
        jnp.exp(score_next - peak_next[:, None]).astype(jnp.bfloat16),
        value_own,
        preferred_element_type=jnp.float32,
    )
    stats = jnp.concatenate(
        [partial_next, peak_next.reshape(-1, HD), total_next.reshape(-1, HD)]
    )
    stats = passed_along(stats, "seq", 1)
    seen = keep_prev[:half] > 0
    got_peak = stats[half : half + half // HD].reshape(half)
    got_total = stats[half + half // HD :].reshape(half)
    rest = tokens - half
    peak_prev = jnp.concatenate(
        [jnp.where(seen, got_peak, NEGATIVE), jnp.full((rest,), NEGATIVE, jnp.float32)]
    )
    total_prev = jnp.concatenate(
        [jnp.where(seen, got_total, 0.0), jnp.zeros((rest,), jnp.float32)]
    )
    partial_prev = jnp.concatenate(
        [jnp.where(seen[:, None], stats[:half], 0.0), jnp.zeros((rest, HD), jnp.float32)]
    )

    highest = jnp.maximum(peak_own, peak_prev)
    scale_own = jnp.exp(peak_own - highest)
    scale_prev = jnp.exp(peak_prev - highest)
    totals = scale_own * total_own + scale_prev * total_prev
    attended = (
        live_rows[:, None]
        * (scale_own[:, None] * partial_own + scale_prev[:, None] * partial_prev)
        / totals[:, None]
    ).astype(jnp.bfloat16)
    row_delta = jnp.sum(cotangent.astype(jnp.float32) * attended.astype(jnp.float32), axis=1)

    control = jnp.stack(
        [
            jnp.where(seen, highest[:half], got_peak),
            jnp.where(seen, 1.0 / totals[:half], 0.0),
            row_delta[:half],
        ]
    )
    control = passed_along(control, "seq", -1)

    weights_own = live_rows[:, None] * jnp.exp(score_own - highest[:, None]) / totals[:, None]
    gq_own, gk_own, gv_own = finish_backward(
        weights_own, cotangent, row_delta, queries, key_own, value_own
    )
    weights_next = jnp.exp(score_next - control[0][:, None]) * control[1][:, None]
    gq_next, gk_next, gv_next = finish_backward(
        weights_next, grad_next, control[2], query_next, key_own, value_own
    )
    gq_prev = passed_along(gq_next, "seq", 1)
    grad_query = (
        gq_own + jnp.concatenate([gq_prev, jnp.zeros((rest, HD), jnp.float32)])
    ).astype(jnp.bfloat16)

    parts = jnp.stack(
        [
            gk_own.astype(jnp.float32) + gk_next.astype(jnp.float32),
            gv_own.astype(jnp.float32) + gv_next.astype(jnp.float32),
        ]
    ).astype(jnp.bfloat16)
    parts = jnp.transpose(parts.reshape(2, rows, copies, groups, HD), (2, 0, 1, 3, 4))
    parts = parts.reshape(blocks, -1)
    summed = lax.psum_scatter(parts, "r", scatter_dimension=0, tiled=True)
    summed = summed.reshape(2, rows, groups, HD)
    returned = lax.all_to_all(summed, "y", split_axis=2, concat_axis=2, tiled=True)
    return (attended, grad_query, returned[0][None], returned[1][None])


def solution(mesh):
    seq_devices, head_devices = mesh.devices.shape
    split = Mesh(
        mesh.devices.reshape(seq_devices, KVH, head_devices // KVH), ("seq", "y", "r")
    )
    heads = ("y", "r")
    return jax.shard_map(
        per_device,
        mesh=split,
        in_specs=(
            P("seq", heads),
            P("seq", heads, None, None),
            P("seq", heads, None, None),
            P("seq", heads),
            P("seq", None),
        ),
        out_specs=(
            P("seq", heads),
            P("seq", heads),
            P("seq", heads, None, None),
            P("seq", heads, None, None),
        ),
        check_vma=False,
    )
```

```python
import jax
import jax.numpy as jnp
from jax import lax
from jax.sharding import Mesh
from jax.sharding import PartitionSpec as P

HD = 128
KVH = 8

NEGATIVE = -1e30


def passed_along(value, axis, by):
    length = lax.axis_size(axis)
    pairs = [(i, i + by) for i in range(length) if 0 <= i + by < length]
    return lax.ppermute(value, axis, pairs)


def block_forward(query_rows, key_rows, value_rows, keep_mask):
    scores = jnp.einsum(
        "rd,kd->rk", query_rows, key_rows, preferred_element_type=jnp.float32
    ) * HD ** (-0.5)
    scores = jnp.where(keep_mask[:, None] > 0, scores, NEGATIVE)
    highest = jnp.max(scores, axis=1)
    powered = jnp.exp(scores - highest[:, None])
    totals = jnp.sum(powered, axis=1)
    partial_value = jnp.dot(
        powered.astype(jnp.bfloat16), value_rows, preferred_element_type=jnp.float32
    )
    return (scores, highest, totals, partial_value)


def finish_backward(weights, grad_rows, row_delta, query_rows, key_rows, value_rows):
    grad_weights = jnp.einsum(
        "rd,kd->rk", grad_rows, value_rows, preferred_element_type=jnp.float32
    )
    grad_scores = (weights * (grad_weights - row_delta[:, None]) * HD ** (-0.5)).astype(
        jnp.bfloat16
    )
    query_grad = jnp.dot(grad_scores, key_rows, preferred_element_type=jnp.float32)
    key_part = jnp.einsum(
        "rk,rd->kd", grad_scores, query_rows, preferred_element_type=jnp.float32
    ).astype(jnp.bfloat16)
    value_part = jnp.einsum(
        "rk,rd->kd", weights.astype(jnp.bfloat16), grad_rows, preferred_element_type=jnp.float32
    ).astype(jnp.bfloat16)
    return (query_grad, key_part, value_part)


def per_device(queries, keys, values, cotangent, mask):
    groups = lax.axis_size("y")
    copies = lax.axis_size("r")
    blocks = groups * copies
    rows = keys.shape[1]
    tokens = queries.shape[0]
    half = tokens // 2

    served = passed_along(jnp.stack([queries[:half], cotangent[:half]]), "seq", -1)
    query_next, grad_next = served[0], served[1]

    own_kv = jnp.stack([keys[0], values[0]])
    own_kv = jnp.transpose(own_kv, (0, 2, 1, 3)).reshape(2, KVH, rows * HD)
    by_group = lax.all_to_all(own_kv, "y", split_axis=1, concat_axis=1, tiled=True)
    gathered = lax.all_gather(by_group, "r", axis=1, tiled=True)
    gathered = jnp.transpose(gathered.reshape(2, blocks, rows, HD), (0, 2, 1, 3))
    gathered = gathered.reshape(2, rows * blocks, HD)
    key_own, value_own = gathered[0], gathered[1]

    keep_own = mask[:, 0]
    keep_prev = mask[:, 1]
    live_rows = (keep_own + keep_prev > 0).astype(jnp.float32)
    score_own, peak_own, total_own, partial_own = block_forward(
        queries, key_own, value_own, keep_own
    )

    score_next = jnp.einsum(
        "rd,kd->rk", query_next, key_own, preferred_element_type=jnp.float32
    ) * HD ** (-0.5)
    peak_next = jnp.max(score_next, axis=1)
    total_next = jnp.sum(jnp.exp(score_next - peak_next[:, None]), axis=1)
    partial_next = jnp.dot(
        jnp.exp(score_next - peak_next[:, None]).astype(jnp.bfloat16),
        value_own,
        preferred_element_type=jnp.float32,
    )
    stats = jnp.concatenate(
        [partial_next, peak_next.reshape(-1, HD), total_next.reshape(-1, HD)]
    )
    stats = passed_along(stats, "seq", 1)
    seen = keep_prev[:half] > 0
    got_peak = stats[half : half + half // HD].reshape(half)
    got_total = stats[half + half // HD :].reshape(half)
    rest = tokens - half
    peak_prev = jnp.concatenate(
        [jnp.where(seen, got_peak, NEGATIVE), jnp.full((rest,), NEGATIVE, jnp.float32)]
    )
    total_prev = jnp.concatenate(
        [jnp.where(seen, got_total, 0.0), jnp.zeros((rest,), jnp.float32)]
    )
    partial_prev = jnp.concatenate(
        [jnp.where(seen[:, None], stats[:half], 0.0), jnp.zeros((rest, HD), jnp.float32)]
    )

    highest = jnp.maximum(peak_own, peak_prev)
    scale_own = jnp.exp(peak_own - highest)
    scale_prev = jnp.exp(peak_prev - highest)
    totals = scale_own * total_own + scale_prev * total_prev
    attended = (
        live_rows[:, None]
        * (scale_own[:, None] * partial_own + scale_prev[:, None] * partial_prev)
        / totals[:, None]
    ).astype(jnp.bfloat16)
    row_delta = jnp.sum(cotangent.astype(jnp.float32) * attended.astype(jnp.float32), axis=1)

    control = jnp.stack(
        [
            jnp.where(seen, highest[:half], got_peak),
            jnp.where(seen, 1.0 / totals[:half], 0.0),
            row_delta[:half],
        ]
    )
    control = passed_along(control, "seq", -1)

    weights_own = live_rows[:, None] * jnp.exp(score_own - highest[:, None]) / totals[:, None]
    gq_own, gk_own, gv_own = finish_backward(
        weights_own, cotangent, row_delta, queries, key_own, value_own
    )
    weights_next = jnp.exp(score_next - control[0][:, None]) * control[1][:, None]
    gq_next, gk_next, gv_next = finish_backward(
        weights_next, grad_next, control[2], query_next, key_own, value_own
    )
    gq_prev = passed_along(gq_next, "seq", 1)
    grad_query = (
        gq_own + jnp.concatenate([gq_prev, jnp.zeros((rest, HD), jnp.float32)])
    ).astype(jnp.bfloat16)

    parts = jnp.stack(
        [
            gk_own.astype(jnp.float32) + gk_next.astype(jnp.float32),
            gv_own.astype(jnp.float32) + gv_next.astype(jnp.float32),
        ]
    ).astype(jnp.bfloat16)
    parts = jnp.transpose(parts.reshape(2, rows, copies, groups, HD), (2, 0, 1, 3, 4))
    parts = lax.all_to_all(parts, "r", split_axis=0, concat_axis=0, tiled=True)
    summed = jnp.sum(parts.astype(jnp.float32), axis=0).astype(jnp.bfloat16)
    returned = lax.all_to_all(summed, "y", split_axis=2, concat_axis=2, tiled=True)
    return (attended, grad_query, returned[0][None], returned[1][None])


def solution(mesh):
    seq_devices, head_devices = mesh.devices.shape
    split = Mesh(
        mesh.devices.reshape(seq_devices, KVH, head_devices // KVH), ("seq", "y", "r")
    )
    heads = ("y", "r")
    return jax.shard_map(
        per_device,
        mesh=split,
        in_specs=(
            P("seq", heads),
            P("seq", heads, None, None),
            P("seq", heads, None, None),
            P("seq", heads),
            P("seq", None),
        ),
        out_specs=(
            P("seq", heads),
            P("seq", heads),
            P("seq", heads, None, None),
            P("seq", heads, None, None),
        ),
        check_vma=False,
    )
```

```python
import jax
import jax.numpy as jnp
from jax import lax
from jax.sharding import Mesh
from jax.sharding import PartitionSpec as P

HD = 128
KVH = 8

NEGATIVE = -1e30


def passed_along(value, axis, by):
    length = lax.axis_size(axis)
    pairs = [(i, i + by) for i in range(length) if 0 <= i + by < length]
    return lax.ppermute(value, axis, pairs)


def partner(value):
    return lax.ppermute(value, "c", [(0, 1), (1, 0)])


def block_forward(query_rows, key_rows, value_rows, keep_mask):
    scores = jnp.einsum(
        "rd,kd->rk", query_rows, key_rows, preferred_element_type=jnp.float32
    ) * HD ** (-0.5)
    scores = jnp.where(keep_mask[:, None] > 0, scores, NEGATIVE)
    highest = jnp.max(scores, axis=1)
    powered = jnp.exp(scores - highest[:, None])
    totals = jnp.sum(powered, axis=1)
    partial_value = jnp.dot(
        powered.astype(jnp.bfloat16), value_rows, preferred_element_type=jnp.float32
    )
    return (scores, highest, totals, partial_value)


def finish_backward(weights, grad_rows, row_delta, query_rows, key_rows, value_rows):
    grad_weights = jnp.einsum(
        "rd,kd->rk", grad_rows, value_rows, preferred_element_type=jnp.float32
    )
    grad_scores = (weights * (grad_weights - row_delta[:, None]) * HD ** (-0.5)).astype(
        jnp.bfloat16
    )
    query_grad = jnp.dot(grad_scores, key_rows, preferred_element_type=jnp.float32)
    key_part = jnp.einsum(
        "rk,rd->kd", grad_scores, query_rows, preferred_element_type=jnp.float32
    ).astype(jnp.bfloat16)
    value_part = jnp.einsum(
        "rk,rd->kd", weights.astype(jnp.bfloat16), grad_rows, preferred_element_type=jnp.float32
    ).astype(jnp.bfloat16)
    return (query_grad, key_part, value_part)


def per_device(queries, keys, values, cotangent, mask):
    groups = lax.axis_size("y")
    far = lax.axis_size("xh")
    blocks = groups * far * lax.axis_size("c")
    rows = keys.shape[1]
    tokens = queries.shape[0]
    half = tokens // 2

    served = passed_along(jnp.stack([queries[:half], cotangent[:half]]), "seq", -1)
    query_next, grad_next = served[0], served[1]

    own_kv = jnp.stack([keys[0], values[0]])
    own_kv = jnp.transpose(own_kv, (0, 2, 1, 3)).reshape(2, KVH, rows * HD)
    by_group = lax.all_to_all(own_kv, "y", split_axis=1, concat_axis=1, tiled=True)
    across = lax.all_gather(by_group, "xh", axis=1, tiled=True)
    gathered = jnp.concatenate([across, partner(across)], axis=1)
    gathered = jnp.transpose(gathered.reshape(2, blocks, rows, HD), (0, 2, 1, 3))
    gathered = gathered.reshape(2, rows * blocks, HD)
    key_own, value_own = gathered[0], gathered[1]

    keep_own = mask[:, 0]
    keep_prev = mask[:, 1]
    live_rows = (keep_own + keep_prev > 0).astype(jnp.float32)
    score_own, peak_own, total_own, partial_own = block_forward(
        queries, key_own, value_own, keep_own
    )

    score_next = jnp.einsum(
        "rd,kd->rk", query_next, key_own, preferred_element_type=jnp.float32
    ) * HD ** (-0.5)
    peak_next = jnp.max(score_next, axis=1)
    total_next = jnp.sum(jnp.exp(score_next - peak_next[:, None]), axis=1)
    partial_next = jnp.dot(
        jnp.exp(score_next - peak_next[:, None]).astype(jnp.bfloat16),
        value_own,
        preferred_element_type=jnp.float32,
    )
    stats = jnp.concatenate(
        [partial_next, peak_next.reshape(-1, HD), total_next.reshape(-1, HD)]
    )
    stats = passed_along(stats, "seq", 1)
    seen = keep_prev[:half] > 0
    got_peak = stats[half : half + half // HD].reshape(half)
    got_total = stats[half + half // HD :].reshape(half)
    rest = tokens - half
    peak_prev = jnp.concatenate(
        [jnp.where(seen, got_peak, NEGATIVE), jnp.full((rest,), NEGATIVE, jnp.float32)]
    )
    total_prev = jnp.concatenate(
        [jnp.where(seen, got_total, 0.0), jnp.zeros((rest,), jnp.float32)]
    )
    partial_prev = jnp.concatenate(
        [jnp.where(seen[:, None], stats[:half], 0.0), jnp.zeros((rest, HD), jnp.float32)]
    )

    highest = jnp.maximum(peak_own, peak_prev)
    scale_own = jnp.exp(peak_own - highest)
    scale_prev = jnp.exp(peak_prev - highest)
    totals = scale_own * total_own + scale_prev * total_prev
    attended = (
        live_rows[:, None]
        * (scale_own[:, None] * partial_own + scale_prev[:, None] * partial_prev)
        / totals[:, None]
    ).astype(jnp.bfloat16)
    row_delta = jnp.sum(cotangent.astype(jnp.float32) * attended.astype(jnp.float32), axis=1)

    control = jnp.stack(
        [
            jnp.where(seen, highest[:half], got_peak),
            jnp.where(seen, 1.0 / totals[:half], 0.0),
            row_delta[:half],
        ]
    )
    control = passed_along(control, "seq", -1)

    weights_own = live_rows[:, None] * jnp.exp(score_own - highest[:, None]) / totals[:, None]
    gq_own, gk_own, gv_own = finish_backward(
        weights_own, cotangent, row_delta, queries, key_own, value_own
    )
    weights_next = jnp.exp(score_next - control[0][:, None]) * control[1][:, None]
    gq_next, gk_next, gv_next = finish_backward(
        weights_next, grad_next, control[2], query_next, key_own, value_own
    )
    gq_prev = passed_along(gq_next, "seq", 1)
    grad_query = (
        gq_own + jnp.concatenate([gq_prev, jnp.zeros((rest, HD), jnp.float32)])
    ).astype(jnp.bfloat16)

    parts = jnp.stack(
        [
            gk_own.astype(jnp.float32) + gk_next.astype(jnp.float32),
            gv_own.astype(jnp.float32) + gv_next.astype(jnp.float32),
        ]
    ).astype(jnp.bfloat16)
    parts = parts.reshape(2, rows, 2, far, groups, HD)
    summed = parts[:, :, 0].astype(jnp.float32) + partner(parts[:, :, 1]).astype(jnp.float32)
    summed = jnp.transpose(summed.astype(jnp.bfloat16), (2, 0, 1, 3, 4))
    summed = lax.all_to_all(summed, "xh", split_axis=0, concat_axis=0, tiled=True)
    summed = jnp.sum(summed.astype(jnp.float32), axis=0).astype(jnp.bfloat16)
    summed = jnp.transpose(summed, (2, 0, 1, 3))
    returned = lax.all_to_all(summed, "y", split_axis=0, concat_axis=0, tiled=True)
    returned = jnp.transpose(returned, (1, 2, 0, 3))
    return (attended, grad_query, returned[0][None], returned[1][None])


def solution(mesh):
    seq_devices, head_devices = mesh.devices.shape
    split = Mesh(
        mesh.devices.reshape(seq_devices, KVH, head_devices // KVH // 2, 2),
        ("seq", "y", "xh", "c"),
    )
    heads = ("y", "xh", "c")
    return jax.shard_map(
        per_device,
        mesh=split,
        in_specs=(
            P("seq", heads),
            P("seq", heads, None, None),
            P("seq", heads, None, None),
            P("seq", heads),
            P("seq", None),
        ),
        out_specs=(
            P("seq", heads),
            P("seq", heads),
            P("seq", heads, None, None),
            P("seq", heads, None, None),
        ),
        check_vma=False,
    )
```

```python
import jax
import jax.numpy as jnp
from jax import lax
from jax.sharding import Mesh
from jax.sharding import PartitionSpec as P

HD = 128
KVH = 8

NEGATIVE = -1e30


def passed_along(value, axis, by):
    length = lax.axis_size(axis)
    pairs = [(i, i + by) for i in range(length) if 0 <= i + by < length]
    return lax.ppermute(value, axis, pairs)


def shifted(value, axis, by):
    length = lax.axis_size(axis)
    return lax.ppermute(value, axis, [(i, (i + by) % length) for i in range(length)])


def partner(value):
    return lax.ppermute(value, "c", [(0, 1), (1, 0)])


def block_forward(query_rows, key_rows, value_rows, keep_mask):
    scores = jnp.einsum(
        "rd,kd->rk", query_rows, key_rows, preferred_element_type=jnp.float32
    ) * HD ** (-0.5)
    scores = jnp.where(keep_mask[:, None] > 0, scores, NEGATIVE)
    highest = jnp.max(scores, axis=1)
    powered = jnp.exp(scores - highest[:, None])
    totals = jnp.sum(powered, axis=1)
    partial_value = jnp.dot(
        powered.astype(jnp.bfloat16), value_rows, preferred_element_type=jnp.float32
    )
    return (scores, highest, totals, partial_value)


def finish_backward(weights, grad_rows, row_delta, query_rows, key_rows, value_rows):
    grad_weights = jnp.einsum(
        "rd,kd->rk", grad_rows, value_rows, preferred_element_type=jnp.float32
    )
    grad_scores = (weights * (grad_weights - row_delta[:, None]) * HD ** (-0.5)).astype(
        jnp.bfloat16
    )
    query_grad = jnp.dot(grad_scores, key_rows, preferred_element_type=jnp.float32)
    key_part = jnp.einsum(
        "rk,rd->kd", grad_scores, query_rows, preferred_element_type=jnp.float32
    ).astype(jnp.bfloat16)
    value_part = jnp.einsum(
        "rk,rd->kd", weights.astype(jnp.bfloat16), grad_rows, preferred_element_type=jnp.float32
    ).astype(jnp.bfloat16)
    return (query_grad, key_part, value_part)


def per_device(queries, keys, values, cotangent, mask):
    groups = lax.axis_size("y")
    blocks = groups * lax.axis_size("xh") * lax.axis_size("c")
    rows = keys.shape[1]
    tokens = queries.shape[0]
    half = tokens // 2

    served = passed_along(jnp.stack([queries[:half], cotangent[:half]]), "seq", -1)
    query_next, grad_next = served[0], served[1]

    own_kv = jnp.stack([keys[0], values[0]])
    own_kv = jnp.transpose(own_kv, (0, 2, 1, 3)).reshape(2, KVH, rows * HD)
    by_group = lax.all_to_all(own_kv, "y", split_axis=1, concat_axis=1, tiled=True)
    far = lax.axis_size("xh")
    across = jnp.concatenate(
        [by_group] + [shifted(by_group, "xh", k) for k in range(1, far)], axis=1
    )
    gathered = jnp.concatenate([across, partner(across)], axis=1)
    gathered = jnp.transpose(gathered.reshape(2, blocks, rows, HD), (0, 2, 1, 3))
    gathered = gathered.reshape(2, rows * blocks, HD)
    key_own, value_own = gathered[0], gathered[1]

    keep_own = mask[:, 0]
    keep_prev = mask[:, 1]
    live_rows = (keep_own + keep_prev > 0).astype(jnp.float32)
    score_own, peak_own, total_own, partial_own = block_forward(
        queries, key_own, value_own, keep_own
    )

    score_next = jnp.einsum(
        "rd,kd->rk", query_next, key_own, preferred_element_type=jnp.float32
    ) * HD ** (-0.5)
    peak_next = jnp.max(score_next, axis=1)
    total_next = jnp.sum(jnp.exp(score_next - peak_next[:, None]), axis=1)
    partial_next = jnp.dot(
        jnp.exp(score_next - peak_next[:, None]).astype(jnp.bfloat16),
        value_own,
        preferred_element_type=jnp.float32,
    )
    stats = jnp.concatenate(
        [partial_next, peak_next.reshape(-1, HD), total_next.reshape(-1, HD)]
    )
    stats = passed_along(stats, "seq", 1)
    seen = keep_prev[:half] > 0
    got_peak = stats[half : half + half // HD].reshape(half)
    got_total = stats[half + half // HD :].reshape(half)
    rest = tokens - half
    peak_prev = jnp.concatenate(
        [jnp.where(seen, got_peak, NEGATIVE), jnp.full((rest,), NEGATIVE, jnp.float32)]
    )
    total_prev = jnp.concatenate(
        [jnp.where(seen, got_total, 0.0), jnp.zeros((rest,), jnp.float32)]
    )
    partial_prev = jnp.concatenate(
        [jnp.where(seen[:, None], stats[:half], 0.0), jnp.zeros((rest, HD), jnp.float32)]
    )

    highest = jnp.maximum(peak_own, peak_prev)
    scale_own = jnp.exp(peak_own - highest)
    scale_prev = jnp.exp(peak_prev - highest)
    totals = scale_own * total_own + scale_prev * total_prev
    attended = (
        live_rows[:, None]
        * (scale_own[:, None] * partial_own + scale_prev[:, None] * partial_prev)
        / totals[:, None]
    ).astype(jnp.bfloat16)
    row_delta = jnp.sum(cotangent.astype(jnp.float32) * attended.astype(jnp.float32), axis=1)

    control = jnp.stack(
        [
            jnp.where(seen, highest[:half], got_peak),
            jnp.where(seen, 1.0 / totals[:half], 0.0),
            row_delta[:half],
        ]
    )
    control = passed_along(control, "seq", -1)

    weights_own = live_rows[:, None] * jnp.exp(score_own - highest[:, None]) / totals[:, None]
    gq_own, gk_own, gv_own = finish_backward(
        weights_own, cotangent, row_delta, queries, key_own, value_own
    )
    weights_next = jnp.exp(score_next - control[0][:, None]) * control[1][:, None]
    gq_next, gk_next, gv_next = finish_backward(
        weights_next, grad_next, control[2], query_next, key_own, value_own
    )
    gq_prev = passed_along(gq_next, "seq", 1)
    grad_query = (
        gq_own + jnp.concatenate([gq_prev, jnp.zeros((rest, HD), jnp.float32)])
    ).astype(jnp.bfloat16)

    parts = jnp.stack(
        [
            gk_own.astype(jnp.float32) + gk_next.astype(jnp.float32),
            gv_own.astype(jnp.float32) + gv_next.astype(jnp.float32),
        ]
    ).astype(jnp.bfloat16)
    parts = parts.reshape(2, rows, 2, far, groups, HD)
    summed = parts[:, :, 0].astype(jnp.float32) + partner(parts[:, :, 1]).astype(jnp.float32)
    summed = summed.astype(jnp.bfloat16)
    total = summed[:, :, 0].astype(jnp.float32)
    for k in range(1, far):
        total = total + shifted(summed[:, :, k], "xh", -k).astype(jnp.float32)
    summed = total.astype(jnp.bfloat16)
    summed = jnp.transpose(summed, (2, 0, 1, 3))
    returned = lax.all_to_all(summed, "y", split_axis=0, concat_axis=0, tiled=True)
    returned = jnp.transpose(returned, (1, 2, 0, 3))
    return (attended, grad_query, returned[0][None], returned[1][None])


def solution(mesh):
    seq_devices, head_devices = mesh.devices.shape
    split = Mesh(
        mesh.devices.reshape(seq_devices, KVH, head_devices // KVH // 2, 2),
        ("seq", "y", "xh", "c"),
    )
    heads = ("y", "xh", "c")
    return jax.shard_map(
        per_device,
        mesh=split,
        in_specs=(
            P("seq", heads),
            P("seq", heads, None, None),
            P("seq", heads, None, None),
            P("seq", heads),
            P("seq", None),
        ),
        out_specs=(
            P("seq", heads),
            P("seq", heads),
            P("seq", heads, None, None),
            P("seq", heads, None, None),
        ),
        check_vma=False,
    )
```

```python
import jax
import jax.numpy as jnp
from jax import lax
from jax.sharding import Mesh
from jax.sharding import PartitionSpec as P

HD = 128
KVH = 8

NEGATIVE = -1e30


def passed_along(value, axis, by):
    length = lax.axis_size(axis)
    pairs = [(i, i + by) for i in range(length) if 0 <= i + by < length]
    return lax.ppermute(value, axis, pairs)


def partner(value):
    return lax.ppermute(value, "c", [(0, 1), (1, 0)])


def block_forward(query_rows, key_rows, value_rows, keep_mask):
    scores = jnp.einsum(
        "rd,kd->rk", query_rows, key_rows, preferred_element_type=jnp.float32
    ) * HD ** (-0.5)
    scores = jnp.where(keep_mask[:, None] > 0, scores, NEGATIVE)
    highest = jnp.max(scores, axis=1)
    powered = jnp.exp(scores - highest[:, None])
    totals = jnp.sum(powered, axis=1)
    partial_value = jnp.dot(
        powered.astype(jnp.bfloat16), value_rows, preferred_element_type=jnp.float32
    )
    return (scores, highest, totals, partial_value)


def finish_backward(weights, grad_rows, row_delta, query_rows, key_rows, value_rows):
    grad_weights = jnp.einsum(
        "rd,kd->rk", grad_rows, value_rows, preferred_element_type=jnp.float32
    )
    grad_scores = (weights * (grad_weights - row_delta[:, None]) * HD ** (-0.5)).astype(
        jnp.bfloat16
    )
    query_grad = jnp.dot(grad_scores, key_rows, preferred_element_type=jnp.float32)
    key_part = jnp.einsum(
        "rk,rd->kd", grad_scores, query_rows, preferred_element_type=jnp.float32
    ).astype(jnp.bfloat16)
    value_part = jnp.einsum(
        "rk,rd->kd", weights.astype(jnp.bfloat16), grad_rows, preferred_element_type=jnp.float32
    ).astype(jnp.bfloat16)
    return (query_grad, key_part, value_part)


def per_device(queries, keys, values, cotangent, mask):
    groups = lax.axis_size("y")
    blocks = groups * lax.axis_size("xh") * lax.axis_size("c")
    rows = keys.shape[1]
    tokens = queries.shape[0]
    half = tokens // 2

    served = passed_along(jnp.stack([queries[:half], cotangent[:half]]), "seq", -1)
    query_next, grad_next = served[0], served[1]

    own_kv = jnp.stack([keys[0], values[0]])
    far = lax.axis_size("xh")
    own_kv = jnp.transpose(own_kv, (2, 0, 1, 3)).reshape(KVH, 1, 2, rows * HD)
    own_kv = jnp.broadcast_to(own_kv, (KVH, far, 2, rows * HD)).reshape(-1, 2, rows * HD)
    across = lax.all_to_all(own_kv, ("y", "xh"), split_axis=0, concat_axis=0, tiled=True)
    across = jnp.transpose(across, (1, 0, 2))
    gathered = jnp.concatenate([across, partner(across)], axis=1)
    gathered = jnp.transpose(gathered.reshape(2, blocks, rows, HD), (0, 2, 1, 3))
    gathered = gathered.reshape(2, rows * blocks, HD)
    key_own, value_own = gathered[0], gathered[1]

    keep_own = mask[:, 0]
    keep_prev = mask[:, 1]
    live_rows = (keep_own + keep_prev > 0).astype(jnp.float32)
    score_own, peak_own, total_own, partial_own = block_forward(
        queries, key_own, value_own, keep_own
    )

    score_next = jnp.einsum(
        "rd,kd->rk", query_next, key_own, preferred_element_type=jnp.float32
    ) * HD ** (-0.5)
    peak_next = jnp.max(score_next, axis=1)
    total_next = jnp.sum(jnp.exp(score_next - peak_next[:, None]), axis=1)
    partial_next = jnp.dot(
        jnp.exp(score_next - peak_next[:, None]).astype(jnp.bfloat16),
        value_own,
        preferred_element_type=jnp.float32,
    )
    stats = jnp.concatenate(
        [partial_next, peak_next.reshape(-1, HD), total_next.reshape(-1, HD)]
    )
    stats = passed_along(stats, "seq", 1)
    seen = keep_prev[:half] > 0
    got_peak = stats[half : half + half // HD].reshape(half)
    got_total = stats[half + half // HD :].reshape(half)
    rest = tokens - half
    peak_prev = jnp.concatenate(
        [jnp.where(seen, got_peak, NEGATIVE), jnp.full((rest,), NEGATIVE, jnp.float32)]
    )
    total_prev = jnp.concatenate(
        [jnp.where(seen, got_total, 0.0), jnp.zeros((rest,), jnp.float32)]
    )
    partial_prev = jnp.concatenate(
        [jnp.where(seen[:, None], stats[:half], 0.0), jnp.zeros((rest, HD), jnp.float32)]
    )

    highest = jnp.maximum(peak_own, peak_prev)
    scale_own = jnp.exp(peak_own - highest)
    scale_prev = jnp.exp(peak_prev - highest)
    totals = scale_own * total_own + scale_prev * total_prev
    attended = (
        live_rows[:, None]
        * (scale_own[:, None] * partial_own + scale_prev[:, None] * partial_prev)
        / totals[:, None]
    ).astype(jnp.bfloat16)
    row_delta = jnp.sum(cotangent.astype(jnp.float32) * attended.astype(jnp.float32), axis=1)

    control = jnp.stack(
        [
            jnp.where(seen, highest[:half], got_peak),
            jnp.where(seen, 1.0 / totals[:half], 0.0),
            row_delta[:half],
        ]
    )
    control = passed_along(control, "seq", -1)

    weights_own = live_rows[:, None] * jnp.exp(score_own - highest[:, None]) / totals[:, None]
    gq_own, gk_own, gv_own = finish_backward(
        weights_own, cotangent, row_delta, queries, key_own, value_own
    )
    weights_next = jnp.exp(score_next - control[0][:, None]) * control[1][:, None]
    gq_next, gk_next, gv_next = finish_backward(
        weights_next, grad_next, control[2], query_next, key_own, value_own
    )
    gq_prev = passed_along(gq_next, "seq", 1)
    grad_query = (
        gq_own + jnp.concatenate([gq_prev, jnp.zeros((rest, HD), jnp.float32)])
    ).astype(jnp.bfloat16)

    parts = jnp.stack(
        [
            gk_own.astype(jnp.float32) + gk_next.astype(jnp.float32),
            gv_own.astype(jnp.float32) + gv_next.astype(jnp.float32),
        ]
    ).astype(jnp.bfloat16)
    parts = parts.reshape(2, rows, 2, groups, far, HD)
    summed = parts[:, :, 0].astype(jnp.float32) + partner(parts[:, :, 1]).astype(jnp.float32)
    summed = jnp.transpose(summed.astype(jnp.bfloat16), (2, 3, 0, 1, 4))
    summed = summed.reshape(groups * far, 2, rows, HD)
    summed = lax.all_to_all(summed, ("y", "xh"), split_axis=0, concat_axis=0, tiled=True)
    summed = summed.reshape(KVH, far, 2, rows, HD).astype(jnp.float32).sum(axis=1)
    returned = jnp.transpose(summed, (1, 2, 0, 3)).astype(jnp.bfloat16)
    return (attended, grad_query, returned[0][None], returned[1][None])


def solution(mesh):
    seq_devices, head_devices = mesh.devices.shape
    split = Mesh(
        mesh.devices.reshape(seq_devices, KVH, head_devices // KVH // 2, 2),
        ("seq", "y", "xh", "c"),
    )
    heads = ("y", "xh", "c")
    return jax.shard_map(
        per_device,
        mesh=split,
        in_specs=(
            P("seq", heads),
            P("seq", heads, None, None),
            P("seq", heads, None, None),
            P("seq", heads),
            P("seq", None),
        ),
        out_specs=(
            P("seq", heads),
            P("seq", heads),
            P("seq", heads, None, None),
            P("seq", heads, None, None),
        ),
        check_vma=False,
    )
```

```python
import jax
import jax.numpy as jnp
from jax import lax
from jax.sharding import Mesh
from jax.sharding import PartitionSpec as P

HD = 128
KVH = 8

NEGATIVE = -1e30


def passed_along(value, axis, by):
    length = lax.axis_size(axis)
    pairs = [(i, i + by) for i in range(length) if 0 <= i + by < length]
    return lax.ppermute(value, axis, pairs)


def partner(value):
    return lax.ppermute(value, "c", [(0, 1), (1, 0)])


def block_forward(query_rows, key_rows, value_rows, keep_mask):
    scores = jnp.einsum(
        "rd,kd->rk", query_rows, key_rows, preferred_element_type=jnp.float32
    ) * HD ** (-0.5)
    scores = jnp.where(keep_mask[:, None] > 0, scores, NEGATIVE)
    highest = jnp.max(scores, axis=1)
    powered = jnp.exp(scores - highest[:, None])
    totals = jnp.sum(powered, axis=1)
    partial_value = jnp.dot(
        powered.astype(jnp.bfloat16), value_rows, preferred_element_type=jnp.float32
    )
    return (scores, highest, totals, partial_value)


def finish_backward(weights, grad_rows, row_delta, query_rows, key_rows, value_rows):
    grad_weights = jnp.einsum(
        "rd,kd->rk", grad_rows, value_rows, preferred_element_type=jnp.float32
    )
    grad_scores = (weights * (grad_weights - row_delta[:, None]) * HD ** (-0.5)).astype(
        jnp.bfloat16
    )
    query_grad = jnp.dot(grad_scores, key_rows, preferred_element_type=jnp.float32)
    key_part = jnp.einsum(
        "rk,rd->kd", grad_scores, query_rows, preferred_element_type=jnp.float32
    ).astype(jnp.bfloat16)
    value_part = jnp.einsum(
        "rk,rd->kd", weights.astype(jnp.bfloat16), grad_rows, preferred_element_type=jnp.float32
    ).astype(jnp.bfloat16)
    return (query_grad, key_part, value_part)


def per_device(queries, keys, values, cotangent, mask):
    groups = lax.axis_size("y")
    blocks = groups * lax.axis_size("xh") * lax.axis_size("c")
    rows = keys.shape[1]
    tokens = queries.shape[0]
    half = tokens // 2

    flags = mask[:half].astype(jnp.bfloat16)
    served = jnp.stack(
        [
            jnp.concatenate([queries[:half], flags[:, 0].reshape(-1, HD)]),
            jnp.concatenate([cotangent[:half], flags[:, 1].reshape(-1, HD)]),
        ]
    )
    served = passed_along(served, "seq", -1)
    query_next, grad_next = served[0, :half], served[1, :half]
    keep_own_next = served[0, half:].reshape(half).astype(jnp.float32)
    keep_prev_next = served[1, half:].reshape(half).astype(jnp.float32)

    own_kv = jnp.stack([keys[0], values[0]])
    far = lax.axis_size("xh")
    own_kv = jnp.transpose(own_kv, (2, 0, 1, 3)).reshape(KVH, 1, 2, rows * HD)
    own_kv = jnp.broadcast_to(own_kv, (KVH, far, 2, rows * HD)).reshape(-1, 2, rows * HD)
    across = lax.all_to_all(own_kv, ("y", "xh"), split_axis=0, concat_axis=0, tiled=True)
    across = jnp.transpose(across, (1, 0, 2))
    gathered = jnp.concatenate([across, partner(across)], axis=1)
    gathered = jnp.transpose(gathered.reshape(2, blocks, rows, HD), (0, 2, 1, 3))
    gathered = gathered.reshape(2, rows * blocks, HD)
    key_own, value_own = gathered[0], gathered[1]

    keep_own = mask[:, 0]
    keep_prev = mask[:, 1]
    live_rows = (keep_own + keep_prev > 0).astype(jnp.float32)
    score_own, peak_own, total_own, partial_own = block_forward(
        queries, key_own, value_own, keep_own
    )

    score_next = jnp.einsum(
        "rd,kd->rk", query_next, key_own, preferred_element_type=jnp.float32
    ) * HD ** (-0.5)
    peak_next = jnp.max(score_next, axis=1)
    total_next = jnp.sum(jnp.exp(score_next - peak_next[:, None]), axis=1)
    partial_next = jnp.dot(
        jnp.exp(score_next - peak_next[:, None]).astype(jnp.bfloat16),
        value_own,
        preferred_element_type=jnp.float32,
    )
    stats = jnp.concatenate(
        [partial_next, peak_next.reshape(-1, HD), total_next.reshape(-1, HD)]
    )
    stats = passed_along(stats, "seq", 1)
    seen = keep_prev[:half] > 0
    got_peak = stats[half : half + half // HD].reshape(half)
    got_total = stats[half + half // HD :].reshape(half)
    rest = tokens - half
    peak_prev = jnp.concatenate(
        [jnp.where(seen, got_peak, NEGATIVE), jnp.full((rest,), NEGATIVE, jnp.float32)]
    )
    total_prev = jnp.concatenate(
        [jnp.where(seen, got_total, 0.0), jnp.zeros((rest,), jnp.float32)]
    )
    partial_prev = jnp.concatenate(
        [jnp.where(seen[:, None], stats[:half], 0.0), jnp.zeros((rest, HD), jnp.float32)]
    )

    highest = jnp.maximum(peak_own, peak_prev)
    scale_own = jnp.exp(peak_own - highest)
    scale_prev = jnp.exp(peak_prev - highest)
    totals = scale_own * total_own + scale_prev * total_prev
    attended = (
        live_rows[:, None]
        * (scale_own[:, None] * partial_own + scale_prev[:, None] * partial_prev)
        / totals[:, None]
    ).astype(jnp.bfloat16)
    row_delta = jnp.sum(cotangent.astype(jnp.float32) * attended.astype(jnp.float32), axis=1)

    mine = jnp.concatenate(
        [partial_own[:half], peak_own[:half].reshape(-1, HD), total_own[:half].reshape(-1, HD)]
    )
    mine = passed_along(mine, "seq", -1)
    seen_next = keep_prev_next > 0
    live_next = (keep_own_next + keep_prev_next > 0).astype(jnp.float32)
    peak_own_next = mine[half : half + half // HD].reshape(half)
    total_own_next = mine[half + half // HD :].reshape(half)
    peak_prev_next = jnp.where(seen_next, peak_next, NEGATIVE)
    highest_next = jnp.maximum(peak_own_next, peak_prev_next)
    scale_own_next = jnp.exp(peak_own_next - highest_next)
    scale_prev_next = jnp.exp(peak_prev_next - highest_next)
    totals_next = scale_own_next * total_own_next + scale_prev_next * jnp.where(
        seen_next, total_next, 0.0
    )
    totals_next = jnp.where(live_next > 0, totals_next, 1.0)
    attended_next = (
        live_next[:, None]
        * (
            scale_own_next[:, None] * mine[:half]
            + scale_prev_next[:, None] * jnp.where(seen_next[:, None], partial_next, 0.0)
        )
        / totals_next[:, None]
    ).astype(jnp.bfloat16)
    delta_next = jnp.sum(
        grad_next.astype(jnp.float32) * attended_next.astype(jnp.float32), axis=1
    )

    weights_own = live_rows[:, None] * jnp.exp(score_own - highest[:, None]) / totals[:, None]
    gq_own, gk_own, gv_own = finish_backward(
        weights_own, cotangent, row_delta, queries, key_own, value_own
    )
    weights_next = jnp.where(
        seen_next[:, None],
        jnp.exp(score_next - highest_next[:, None]) / totals_next[:, None],
        0.0,
    )
    gq_next, gk_next, gv_next = finish_backward(
        weights_next, grad_next, delta_next, query_next, key_own, value_own
    )
    gq_prev = passed_along(gq_next, "seq", 1)
    grad_query = (
        gq_own + jnp.concatenate([gq_prev, jnp.zeros((rest, HD), jnp.float32)])
    ).astype(jnp.bfloat16)

    parts = jnp.stack(
        [
            gk_own.astype(jnp.float32) + gk_next.astype(jnp.float32),
            gv_own.astype(jnp.float32) + gv_next.astype(jnp.float32),
        ]
    ).astype(jnp.bfloat16)
    parts = parts.reshape(2, rows, 2, groups, far, HD)
    summed = parts[:, :, 0].astype(jnp.float32) + partner(parts[:, :, 1]).astype(jnp.float32)
    summed = jnp.transpose(summed.astype(jnp.bfloat16), (2, 3, 0, 1, 4))
    summed = summed.reshape(groups * far, 2, rows, HD)
    summed = lax.all_to_all(summed, ("y", "xh"), split_axis=0, concat_axis=0, tiled=True)
    summed = summed.reshape(KVH, far, 2, rows, HD).astype(jnp.float32).sum(axis=1)
    returned = jnp.transpose(summed, (1, 2, 0, 3)).astype(jnp.bfloat16)
    return (attended, grad_query, returned[0][None], returned[1][None])


def solution(mesh):
    seq_devices, head_devices = mesh.devices.shape
    split = Mesh(
        mesh.devices.reshape(seq_devices, KVH, head_devices // KVH // 2, 2),
        ("seq", "y", "xh", "c"),
    )
    heads = ("y", "xh", "c")
    return jax.shard_map(
        per_device,
        mesh=split,
        in_specs=(
            P("seq", heads),
            P("seq", heads, None, None),
            P("seq", heads, None, None),
            P("seq", heads),
            P("seq", None),
        ),
        out_specs=(
            P("seq", heads),
            P("seq", heads),
            P("seq", heads, None, None),
            P("seq", heads, None, None),
        ),
        check_vma=False,
    )
```

```python
import jax
import jax.numpy as jnp
from jax import lax
from jax.sharding import Mesh
from jax.sharding import PartitionSpec as P

HD = 128
KVH = 8

NEGATIVE = -1e30


def passed_along(value, axis, by):
    length = lax.axis_size(axis)
    pairs = [(i, i + by) for i in range(length) if 0 <= i + by < length]
    return lax.ppermute(value, axis, pairs)


def partner(value):
    return lax.ppermute(value, "c", [(0, 1), (1, 0)])


def block_forward(query_rows, key_rows, value_rows, keep_mask):
    scores = jnp.einsum(
        "rd,kd->rk", query_rows, key_rows, preferred_element_type=jnp.float32
    ) * HD ** (-0.5)
    scores = jnp.where(keep_mask[:, None] > 0, scores, NEGATIVE)
    highest = jnp.max(scores, axis=1)
    powered = jnp.exp(scores - highest[:, None])
    totals = jnp.sum(powered, axis=1)
    partial_value = jnp.dot(
        powered.astype(jnp.bfloat16), value_rows, preferred_element_type=jnp.float32
    )
    return (scores, highest, totals, partial_value)


def finish_backward(weights, grad_rows, row_delta, query_rows, key_rows, value_rows):
    grad_weights = jnp.einsum(
        "rd,kd->rk", grad_rows, value_rows, preferred_element_type=jnp.float32
    )
    grad_scores = (weights * (grad_weights - row_delta[:, None]) * HD ** (-0.5)).astype(
        jnp.bfloat16
    )
    query_grad = jnp.dot(grad_scores, key_rows, preferred_element_type=jnp.float32)
    key_part = jnp.einsum(
        "rk,rd->kd", grad_scores, query_rows, preferred_element_type=jnp.float32
    ).astype(jnp.bfloat16)
    value_part = jnp.einsum(
        "rk,rd->kd", weights.astype(jnp.bfloat16), grad_rows, preferred_element_type=jnp.float32
    ).astype(jnp.bfloat16)
    return (query_grad, key_part, value_part)


def per_device(queries, keys, values, cotangent, mask):
    groups = lax.axis_size("y")
    blocks = groups * lax.axis_size("xh") * lax.axis_size("c")
    rows = keys.shape[1]
    tokens = queries.shape[0]
    half = tokens // 2

    flags = mask[:half].astype(jnp.bfloat16)
    served = jnp.stack(
        [
            jnp.concatenate([queries[:half], flags[:, 0].reshape(-1, HD)]),
            jnp.concatenate([cotangent[:half], flags[:, 1].reshape(-1, HD)]),
        ]
    )
    served = passed_along(served, "seq", -1)
    query_next, grad_next = served[0, :half], served[1, :half]
    keep_own_next = served[0, half:].reshape(half).astype(jnp.float32)
    keep_prev_next = served[1, half:].reshape(half).astype(jnp.float32)

    own_kv = jnp.stack([keys[0], values[0]])
    far = lax.axis_size("xh")
    own_kv = jnp.transpose(own_kv, (2, 0, 1, 3)).reshape(KVH, 1, 2, rows * HD)
    own_kv = jnp.broadcast_to(own_kv, (KVH, far, 2, rows * HD)).reshape(-1, 2, rows * HD)
    across = lax.all_to_all(own_kv, ("y", "xh"), split_axis=0, concat_axis=0, tiled=True)
    across = jnp.transpose(across, (1, 0, 2))
    gathered = jnp.concatenate([across, partner(across)], axis=1)
    gathered = jnp.transpose(gathered.reshape(2, blocks, rows, HD), (0, 2, 1, 3))
    gathered = gathered.reshape(2, rows * blocks, HD)
    key_own, value_own = gathered[0], gathered[1]

    keep_own = mask[:, 0]
    keep_prev = mask[:, 1]
    live_rows = (keep_own + keep_prev > 0).astype(jnp.float32)
    score_own, peak_own, total_own, partial_own = block_forward(
        queries, key_own, value_own, keep_own
    )

    mine = jnp.concatenate(
        [partial_own[:half], peak_own[:half].reshape(-1, HD), total_own[:half].reshape(-1, HD)]
    )
    mine, query_next = lax.optimization_barrier((mine, query_next))
    mine = passed_along(mine, "seq", -1)

    score_next = jnp.einsum(
        "rd,kd->rk", query_next, key_own, preferred_element_type=jnp.float32
    ) * HD ** (-0.5)
    peak_next = jnp.max(score_next, axis=1)
    total_next = jnp.sum(jnp.exp(score_next - peak_next[:, None]), axis=1)
    partial_next = jnp.dot(
        jnp.exp(score_next - peak_next[:, None]).astype(jnp.bfloat16),
        value_own,
        preferred_element_type=jnp.float32,
    )
    stats = jnp.concatenate(
        [partial_next, peak_next.reshape(-1, HD), total_next.reshape(-1, HD)]
    )
    stats = passed_along(stats, "seq", 1)
    seen = keep_prev[:half] > 0
    got_peak = stats[half : half + half // HD].reshape(half)
    got_total = stats[half + half // HD :].reshape(half)
    rest = tokens - half
    peak_prev = jnp.concatenate(
        [jnp.where(seen, got_peak, NEGATIVE), jnp.full((rest,), NEGATIVE, jnp.float32)]
    )
    total_prev = jnp.concatenate(
        [jnp.where(seen, got_total, 0.0), jnp.zeros((rest,), jnp.float32)]
    )
    partial_prev = jnp.concatenate(
        [jnp.where(seen[:, None], stats[:half], 0.0), jnp.zeros((rest, HD), jnp.float32)]
    )

    highest = jnp.maximum(peak_own, peak_prev)
    scale_own = jnp.exp(peak_own - highest)
    scale_prev = jnp.exp(peak_prev - highest)
    totals = scale_own * total_own + scale_prev * total_prev
    attended = (
        live_rows[:, None]
        * (scale_own[:, None] * partial_own + scale_prev[:, None] * partial_prev)
        / totals[:, None]
    ).astype(jnp.bfloat16)
    row_delta = jnp.sum(cotangent.astype(jnp.float32) * attended.astype(jnp.float32), axis=1)

    seen_next = keep_prev_next > 0
    live_next = (keep_own_next + keep_prev_next > 0).astype(jnp.float32)
    peak_own_next = mine[half : half + half // HD].reshape(half)
    total_own_next = mine[half + half // HD :].reshape(half)
    peak_prev_next = jnp.where(seen_next, peak_next, NEGATIVE)
    highest_next = jnp.maximum(peak_own_next, peak_prev_next)
    scale_own_next = jnp.exp(peak_own_next - highest_next)
    scale_prev_next = jnp.exp(peak_prev_next - highest_next)
    totals_next = scale_own_next * total_own_next + scale_prev_next * jnp.where(
        seen_next, total_next, 0.0
    )
    totals_next = jnp.where(live_next > 0, totals_next, 1.0)
    attended_next = (
        live_next[:, None]
        * (
            scale_own_next[:, None] * mine[:half]
            + scale_prev_next[:, None] * jnp.where(seen_next[:, None], partial_next, 0.0)
        )
        / totals_next[:, None]
    ).astype(jnp.bfloat16)
    delta_next = jnp.sum(
        grad_next.astype(jnp.float32) * attended_next.astype(jnp.float32), axis=1
    )

    weights_own = live_rows[:, None] * jnp.exp(score_own - highest[:, None]) / totals[:, None]
    gq_own, gk_own, gv_own = finish_backward(
        weights_own, cotangent, row_delta, queries, key_own, value_own
    )
    weights_next = jnp.where(
        seen_next[:, None],
        jnp.exp(score_next - highest_next[:, None]) / totals_next[:, None],
        0.0,
    )
    gq_next, gk_next, gv_next = finish_backward(
        weights_next, grad_next, delta_next, query_next, key_own, value_own
    )
    gq_prev = passed_along(gq_next, "seq", 1)
    grad_query = (
        gq_own + jnp.concatenate([gq_prev, jnp.zeros((rest, HD), jnp.float32)])
    ).astype(jnp.bfloat16)

    parts = jnp.stack(
        [
            gk_own.astype(jnp.float32) + gk_next.astype(jnp.float32),
            gv_own.astype(jnp.float32) + gv_next.astype(jnp.float32),
        ]
    ).astype(jnp.bfloat16)
    parts = parts.reshape(2, rows, 2, groups, far, HD)
    summed = parts[:, :, 0].astype(jnp.float32) + partner(parts[:, :, 1]).astype(jnp.float32)
    summed = jnp.transpose(summed.astype(jnp.bfloat16), (2, 3, 0, 1, 4))
    summed = summed.reshape(groups * far, 2, rows, HD)
    summed = lax.all_to_all(summed, ("y", "xh"), split_axis=0, concat_axis=0, tiled=True)
    summed = summed.reshape(KVH, far, 2, rows, HD).astype(jnp.float32).sum(axis=1)
    returned = jnp.transpose(summed, (1, 2, 0, 3)).astype(jnp.bfloat16)
    return (attended, grad_query, returned[0][None], returned[1][None])


def solution(mesh):
    seq_devices, head_devices = mesh.devices.shape
    split = Mesh(
        mesh.devices.reshape(seq_devices, KVH, head_devices // KVH // 2, 2),
        ("seq", "y", "xh", "c"),
    )
    heads = ("y", "xh", "c")
    return jax.shard_map(
        per_device,
        mesh=split,
        in_specs=(
            P("seq", heads),
            P("seq", heads, None, None),
            P("seq", heads, None, None),
            P("seq", heads),
            P("seq", None),
        ),
        out_specs=(
            P("seq", heads),
            P("seq", heads),
            P("seq", heads, None, None),
            P("seq", heads, None, None),
        ),
        check_vma=False,
    )
```

```python
import jax
import jax.numpy as jnp
from jax import lax
from jax.sharding import Mesh
from jax.sharding import PartitionSpec as P

HD = 128
KVH = 8

NEGATIVE = -1e30


def passed_along(value, axis, by):
    length = lax.axis_size(axis)
    pairs = [(i, i + by) for i in range(length) if 0 <= i + by < length]
    return lax.ppermute(value, axis, pairs)


def partner(value):
    return lax.ppermute(value, "c", [(0, 1), (1, 0)])


def block_forward(query_rows, key_rows, value_rows, keep_mask):
    scores = jnp.einsum(
        "rd,kd->rk", query_rows, key_rows, preferred_element_type=jnp.float32
    ) * HD ** (-0.5)
    scores = jnp.where(keep_mask[:, None] > 0, scores, NEGATIVE)
    highest = jnp.max(scores, axis=1)
    powered = jnp.exp(scores - highest[:, None])
    totals = jnp.sum(powered, axis=1)
    partial_value = jnp.dot(
        powered.astype(jnp.bfloat16), value_rows, preferred_element_type=jnp.float32
    )
    return (scores, highest, totals, partial_value)


def finish_backward(weights, grad_rows, row_delta, query_rows, key_rows, value_rows):
    grad_weights = jnp.einsum(
        "rd,kd->rk", grad_rows, value_rows, preferred_element_type=jnp.float32
    )
    grad_scores = (weights * (grad_weights - row_delta[:, None]) * HD ** (-0.5)).astype(
        jnp.bfloat16
    )
    query_grad = jnp.dot(grad_scores, key_rows, preferred_element_type=jnp.float32)
    key_part = jnp.einsum(
        "rk,rd->kd", grad_scores, query_rows, preferred_element_type=jnp.float32
    ).astype(jnp.bfloat16)
    value_part = jnp.einsum(
        "rk,rd->kd", weights.astype(jnp.bfloat16), grad_rows, preferred_element_type=jnp.float32
    ).astype(jnp.bfloat16)
    return (query_grad, key_part, value_part)


def per_device(queries, keys, values, cotangent, mask):
    groups = lax.axis_size("y")
    blocks = groups * lax.axis_size("xh") * lax.axis_size("c")
    rows = keys.shape[1]
    tokens = queries.shape[0]
    half = tokens // 2

    flags = mask[:half].astype(jnp.bfloat16)
    served = jnp.stack(
        [
            jnp.concatenate([queries[:half], flags[:, 0].reshape(-1, HD)]),
            jnp.concatenate([cotangent[:half], flags[:, 1].reshape(-1, HD)]),
        ]
    )
    served = passed_along(served, "seq", -1)
    query_next, grad_next = served[0, :half], served[1, :half]
    keep_own_next = served[0, half:].reshape(half).astype(jnp.float32)
    keep_prev_next = served[1, half:].reshape(half).astype(jnp.float32)

    own_kv = jnp.stack([keys[0], values[0]])
    far = lax.axis_size("xh")
    own_kv = jnp.transpose(own_kv, (2, 0, 1, 3)).reshape(KVH, 1, 2, rows * HD)
    own_kv = jnp.broadcast_to(own_kv, (KVH, far, 2, rows * HD)).reshape(-1, 2, rows * HD)
    across = lax.all_to_all(own_kv, ("y", "xh"), split_axis=0, concat_axis=0, tiled=True)
    across = jnp.transpose(across, (1, 0, 2))
    gathered = jnp.concatenate([across, partner(across)], axis=1)
    gathered = jnp.transpose(gathered.reshape(2, blocks, rows, HD), (0, 2, 1, 3))
    gathered = gathered.reshape(2, rows * blocks, HD)
    key_own, value_own = gathered[0], gathered[1]

    keep_own = mask[:, 0]
    keep_prev = mask[:, 1]
    live_rows = (keep_own + keep_prev > 0).astype(jnp.float32)
    score_own, peak_own, total_own, partial_own = block_forward(
        queries, key_own, value_own, keep_own
    )

    score_next = jnp.einsum(
        "rd,kd->rk", query_next, key_own, preferred_element_type=jnp.float32
    ) * HD ** (-0.5)
    peak_next = jnp.max(score_next, axis=1)
    total_next = jnp.sum(jnp.exp(score_next - peak_next[:, None]), axis=1)
    partial_next = jnp.dot(
        jnp.exp(score_next - peak_next[:, None]).astype(jnp.bfloat16),
        value_own,
        preferred_element_type=jnp.float32,
    )
    seen = keep_prev[:half] > 0
    rest = tokens - half
    totals = jnp.where(live_rows > 0, total_own, 1.0)
    attended = (live_rows[:, None] * partial_own / totals[:, None]).astype(jnp.bfloat16)
    row_delta = jnp.sum(cotangent.astype(jnp.float32) * attended.astype(jnp.float32), axis=1)

    mine = jnp.concatenate(
        [partial_own[:half], peak_own[:half].reshape(-1, HD), total_own[:half].reshape(-1, HD)]
    )
    mine = passed_along(mine, "seq", -1)
    seen_next = keep_prev_next > 0
    live_next = (keep_own_next + keep_prev_next > 0).astype(jnp.float32)
    peak_own_next = mine[half : half + half // HD].reshape(half)
    total_own_next = mine[half + half // HD :].reshape(half)
    peak_prev_next = jnp.where(seen_next, peak_next, NEGATIVE)
    highest_next = jnp.maximum(peak_own_next, peak_prev_next)
    scale_own_next = jnp.exp(peak_own_next - highest_next)
    scale_prev_next = jnp.exp(peak_prev_next - highest_next)
    totals_next = scale_own_next * total_own_next + scale_prev_next * jnp.where(
        seen_next, total_next, 0.0
    )
    totals_next = jnp.where(live_next > 0, totals_next, 1.0)
    attended_next = (
        live_next[:, None]
        * (
            scale_own_next[:, None] * mine[:half]
            + scale_prev_next[:, None] * jnp.where(seen_next[:, None], partial_next, 0.0)
        )
        / totals_next[:, None]
    ).astype(jnp.bfloat16)
    delta_next = jnp.sum(
        grad_next.astype(jnp.float32) * attended_next.astype(jnp.float32), axis=1
    )

    weights_next = jnp.where(
        seen_next[:, None],
        jnp.exp(score_next - highest_next[:, None]) / totals_next[:, None],
        0.0,
    )
    gq_next, gk_next, gv_next = finish_backward(
        weights_next, grad_next, delta_next, query_next, key_own, value_own
    )
    back = jnp.concatenate(
        [
            gq_next,
            attended_next.astype(jnp.float32),
            highest_next.reshape(-1, HD),
            totals_next.reshape(-1, HD),
            delta_next.reshape(-1, HD),
        ]
    )
    back = passed_along(back, "seq", 1)
    step = half // HD
    got = [back[2 * half + i * step : 2 * half + (i + 1) * step].reshape(half) for i in range(3)]
    highest = jnp.concatenate([jnp.where(seen, got[0], peak_own[:half]), peak_own[half:]])
    totals = jnp.concatenate([jnp.where(seen, got[1], totals[:half]), totals[half:]])
    row_delta = jnp.concatenate([jnp.where(seen, got[2], row_delta[:half]), row_delta[half:]])
    attended = jnp.concatenate(
        [
            jnp.where(seen[:, None], back[half : 2 * half].astype(jnp.bfloat16), attended[:half]),
            attended[half:],
        ]
    )

    weights_own = live_rows[:, None] * jnp.exp(score_own - highest[:, None]) / totals[:, None]
    gq_own, gk_own, gv_own = finish_backward(
        weights_own, cotangent, row_delta, queries, key_own, value_own
    )
    grad_query = (
        gq_own + jnp.concatenate([back[:half], jnp.zeros((rest, HD), jnp.float32)])
    ).astype(jnp.bfloat16)

    parts = jnp.stack(
        [
            gk_own.astype(jnp.float32) + gk_next.astype(jnp.float32),
            gv_own.astype(jnp.float32) + gv_next.astype(jnp.float32),
        ]
    ).astype(jnp.bfloat16)
    parts = parts.reshape(2, rows, 2, groups, far, HD)
    summed = parts[:, :, 0].astype(jnp.float32) + partner(parts[:, :, 1]).astype(jnp.float32)
    summed = jnp.transpose(summed.astype(jnp.bfloat16), (2, 3, 0, 1, 4))
    summed = summed.reshape(groups * far, 2, rows, HD)
    summed = lax.all_to_all(summed, ("y", "xh"), split_axis=0, concat_axis=0, tiled=True)
    summed = summed.reshape(KVH, far, 2, rows, HD).astype(jnp.float32).sum(axis=1)
    returned = jnp.transpose(summed, (1, 2, 0, 3)).astype(jnp.bfloat16)
    return (attended, grad_query, returned[0][None], returned[1][None])


def solution(mesh):
    seq_devices, head_devices = mesh.devices.shape
    split = Mesh(
        mesh.devices.reshape(seq_devices, KVH, head_devices // KVH // 2, 2),
        ("seq", "y", "xh", "c"),
    )
    heads = ("y", "xh", "c")
    return jax.shard_map(
        per_device,
        mesh=split,
        in_specs=(
            P("seq", heads),
            P("seq", heads, None, None),
            P("seq", heads, None, None),
            P("seq", heads),
            P("seq", None),
        ),
        out_specs=(
            P("seq", heads),
            P("seq", heads),
            P("seq", heads, None, None),
            P("seq", heads, None, None),
        ),
        check_vma=False,
    )
```

```python
import jax
import jax.numpy as jnp
from jax import lax
from jax.sharding import Mesh
from jax.sharding import PartitionSpec as P

HD = 128
KVH = 8

NEGATIVE = -1e30


def passed_along(value, axis, by):
    length = lax.axis_size(axis)
    pairs = [(i, i + by) for i in range(length) if 0 <= i + by < length]
    return lax.ppermute(value, axis, pairs)


def partner(value):
    return lax.ppermute(value, "c", [(0, 1), (1, 0)])


def scores_of(query_rows, key_halves):
    return jnp.concatenate(
        [
            jnp.einsum("rd,kd->rk", query_rows, k, preferred_element_type=jnp.float32)
            for k in key_halves
        ],
        axis=1,
    ) * HD ** (-0.5)


def block_forward(query_rows, key_halves, value_rows, keep_mask):
    scores = scores_of(query_rows, key_halves)
    scores = jnp.where(keep_mask[:, None] > 0, scores, NEGATIVE)
    highest = jnp.max(scores, axis=1)
    powered = jnp.exp(scores - highest[:, None])
    totals = jnp.sum(powered, axis=1)
    partial_value = jnp.dot(
        powered.astype(jnp.bfloat16), value_rows, preferred_element_type=jnp.float32
    )
    return (scores, highest, totals, partial_value)


def finish_backward(weights, grad_rows, row_delta, query_rows, key_rows, value_rows):
    grad_weights = jnp.einsum(
        "rd,kd->rk", grad_rows, value_rows, preferred_element_type=jnp.float32
    )
    grad_scores = (weights * (grad_weights - row_delta[:, None]) * HD ** (-0.5)).astype(
        jnp.bfloat16
    )
    query_grad = jnp.dot(grad_scores, key_rows, preferred_element_type=jnp.float32)
    key_part = jnp.einsum(
        "rk,rd->kd", grad_scores, query_rows, preferred_element_type=jnp.float32
    ).astype(jnp.bfloat16)
    value_part = jnp.einsum(
        "rk,rd->kd", weights.astype(jnp.bfloat16), grad_rows, preferred_element_type=jnp.float32
    ).astype(jnp.bfloat16)
    return (query_grad, key_part, value_part)


def per_device(queries, keys, values, cotangent, mask):
    groups = lax.axis_size("y")
    blocks = groups * lax.axis_size("xh") * lax.axis_size("c")
    rows = keys.shape[1]
    tokens = queries.shape[0]
    half = tokens // 2

    flags = mask[:half].astype(jnp.bfloat16)
    served = jnp.stack(
        [
            jnp.concatenate([queries[:half], flags[:, 0].reshape(-1, HD)]),
            jnp.concatenate([cotangent[:half], flags[:, 1].reshape(-1, HD)]),
        ]
    )
    served = passed_along(served, "seq", -1)
    query_next, grad_next = served[0, :half], served[1, :half]
    keep_own_next = served[0, half:].reshape(half).astype(jnp.float32)
    keep_prev_next = served[1, half:].reshape(half).astype(jnp.float32)

    own_kv = jnp.stack([keys[0], values[0]])
    far = lax.axis_size("xh")
    own_kv = jnp.transpose(own_kv, (2, 0, 1, 3)).reshape(KVH, 1, 2, rows * HD)
    own_kv = jnp.broadcast_to(own_kv, (KVH, far, 2, rows * HD)).reshape(-1, 2, rows * HD)
    across = lax.all_to_all(own_kv, ("y", "xh"), split_axis=0, concat_axis=0, tiled=True)
    across = jnp.transpose(across, (1, 0, 2))
    def rows_of(half_blocks):
        half_blocks = half_blocks.reshape(2, blocks // 2, rows, HD)
        return jnp.transpose(half_blocks, (0, 2, 1, 3)).reshape(2, rows * blocks // 2, HD)

    mine = rows_of(across)
    other = rows_of(partner(across))
    key_halves = (mine[0], other[0])
    key_own = jnp.concatenate(key_halves)
    value_own = jnp.concatenate([mine[1], other[1]])

    keep_own = mask[:, 0]
    keep_prev = mask[:, 1]
    live_rows = (keep_own + keep_prev > 0).astype(jnp.float32)
    score_own, peak_own, total_own, partial_own = block_forward(
        queries, key_halves, value_own, keep_own
    )

    score_next = scores_of(query_next, key_halves)
    peak_next = jnp.max(score_next, axis=1)
    total_next = jnp.sum(jnp.exp(score_next - peak_next[:, None]), axis=1)
    partial_next = jnp.dot(
        jnp.exp(score_next - peak_next[:, None]).astype(jnp.bfloat16),
        value_own,
        preferred_element_type=jnp.float32,
    )
    stats = jnp.concatenate(
        [partial_next, peak_next.reshape(-1, HD), total_next.reshape(-1, HD)]
    )
    stats = passed_along(stats, "seq", 1)
    seen = keep_prev[:half] > 0
    got_peak = stats[half : half + half // HD].reshape(half)
    got_total = stats[half + half // HD :].reshape(half)
    rest = tokens - half
    peak_prev = jnp.concatenate(
        [jnp.where(seen, got_peak, NEGATIVE), jnp.full((rest,), NEGATIVE, jnp.float32)]
    )
    total_prev = jnp.concatenate(
        [jnp.where(seen, got_total, 0.0), jnp.zeros((rest,), jnp.float32)]
    )
    partial_prev = jnp.concatenate(
        [jnp.where(seen[:, None], stats[:half], 0.0), jnp.zeros((rest, HD), jnp.float32)]
    )

    highest = jnp.maximum(peak_own, peak_prev)
    scale_own = jnp.exp(peak_own - highest)
    scale_prev = jnp.exp(peak_prev - highest)
    totals = scale_own * total_own + scale_prev * total_prev
    attended = (
        live_rows[:, None]
        * (scale_own[:, None] * partial_own + scale_prev[:, None] * partial_prev)
        / totals[:, None]
    ).astype(jnp.bfloat16)
    row_delta = jnp.sum(cotangent.astype(jnp.float32) * attended.astype(jnp.float32), axis=1)

    mine = jnp.concatenate(
        [partial_own[:half], peak_own[:half].reshape(-1, HD), total_own[:half].reshape(-1, HD)]
    )
    mine = passed_along(mine, "seq", -1)
    seen_next = keep_prev_next > 0
    live_next = (keep_own_next + keep_prev_next > 0).astype(jnp.float32)
    peak_own_next = mine[half : half + half // HD].reshape(half)
    total_own_next = mine[half + half // HD :].reshape(half)
    peak_prev_next = jnp.where(seen_next, peak_next, NEGATIVE)
    highest_next = jnp.maximum(peak_own_next, peak_prev_next)
    scale_own_next = jnp.exp(peak_own_next - highest_next)
    scale_prev_next = jnp.exp(peak_prev_next - highest_next)
    totals_next = scale_own_next * total_own_next + scale_prev_next * jnp.where(
        seen_next, total_next, 0.0
    )
    totals_next = jnp.where(live_next > 0, totals_next, 1.0)
    attended_next = (
        live_next[:, None]
        * (
            scale_own_next[:, None] * mine[:half]
            + scale_prev_next[:, None] * jnp.where(seen_next[:, None], partial_next, 0.0)
        )
        / totals_next[:, None]
    ).astype(jnp.bfloat16)
    delta_next = jnp.sum(
        grad_next.astype(jnp.float32) * attended_next.astype(jnp.float32), axis=1
    )

    weights_own = live_rows[:, None] * jnp.exp(score_own - highest[:, None]) / totals[:, None]
    gq_own, gk_own, gv_own = finish_backward(
        weights_own, cotangent, row_delta, queries, key_own, value_own
    )
    weights_next = jnp.where(
        seen_next[:, None],
        jnp.exp(score_next - highest_next[:, None]) / totals_next[:, None],
        0.0,
    )
    gq_next, gk_next, gv_next = finish_backward(
        weights_next, grad_next, delta_next, query_next, key_own, value_own
    )
    gq_prev = passed_along(gq_next, "seq", 1)
    grad_query = (
        gq_own + jnp.concatenate([gq_prev, jnp.zeros((rest, HD), jnp.float32)])
    ).astype(jnp.bfloat16)

    parts = jnp.stack(
        [
            gk_own.astype(jnp.float32) + gk_next.astype(jnp.float32),
            gv_own.astype(jnp.float32) + gv_next.astype(jnp.float32),
        ]
    ).astype(jnp.bfloat16)
    parts = parts.reshape(2, 2, rows, groups, far, HD)
    summed = parts[:, 0].astype(jnp.float32) + partner(parts[:, 1]).astype(jnp.float32)
    summed = jnp.transpose(summed.astype(jnp.bfloat16), (2, 3, 0, 1, 4))
    summed = summed.reshape(groups * far, 2, rows, HD)
    summed = lax.all_to_all(summed, ("y", "xh"), split_axis=0, concat_axis=0, tiled=True)
    summed = summed.reshape(KVH, far, 2, rows, HD).astype(jnp.float32).sum(axis=1)
    returned = jnp.transpose(summed, (1, 2, 0, 3)).astype(jnp.bfloat16)
    return (attended, grad_query, returned[0][None], returned[1][None])


def solution(mesh):
    seq_devices, head_devices = mesh.devices.shape
    split = Mesh(
        mesh.devices.reshape(seq_devices, KVH, head_devices // KVH // 2, 2),
        ("seq", "y", "xh", "c"),
    )
    heads = ("y", "xh", "c")
    return jax.shard_map(
        per_device,
        mesh=split,
        in_specs=(
            P("seq", heads),
            P("seq", heads, None, None),
            P("seq", heads, None, None),
            P("seq", heads),
            P("seq", None),
        ),
        out_specs=(
            P("seq", heads),
            P("seq", heads),
            P("seq", heads, None, None),
            P("seq", heads, None, None),
        ),
        check_vma=False,
    )
```

```python
import jax
import jax.numpy as jnp
from jax import lax
from jax.sharding import Mesh
from jax.sharding import PartitionSpec as P

HD = 128
KVH = 8

NEGATIVE = -1e30


def passed_along(value, axis, by):
    length = lax.axis_size(axis)
    pairs = [(i, i + by) for i in range(length) if 0 <= i + by < length]
    return lax.ppermute(value, axis, pairs)


def partner(value):
    return lax.ppermute(value, "c", [(0, 1), (1, 0)])


def block_forward(query_rows, key_rows, value_rows, keep_mask):
    scores = jnp.einsum(
        "rd,kd->rk", query_rows, key_rows, preferred_element_type=jnp.float32
    ) * HD ** (-0.5)
    scores = jnp.where(keep_mask[:, None] > 0, scores, NEGATIVE)
    highest = jnp.max(scores, axis=1)
    powered = jnp.exp(scores - highest[:, None])
    totals = jnp.sum(powered, axis=1)
    partial_value = jnp.dot(
        powered.astype(jnp.bfloat16), value_rows, preferred_element_type=jnp.float32
    )
    return (scores, highest, totals, partial_value)


def finish_backward(
    weights, grad_rows, row_delta, query_rows, key_rows, value_rows, narrow=jnp.bfloat16
):
    grad_weights = jnp.einsum(
        "rd,kd->rk", grad_rows, value_rows, preferred_element_type=jnp.float32
    )
    grad_scores = (weights * (grad_weights - row_delta[:, None]) * HD ** (-0.5)).astype(
        jnp.bfloat16
    )
    query_grad = jnp.dot(grad_scores, key_rows, preferred_element_type=jnp.float32)
    key_part = jnp.einsum(
        "rk,rd->kd", grad_scores, query_rows, preferred_element_type=jnp.float32
    ).astype(narrow)
    value_part = jnp.einsum(
        "rk,rd->kd", weights.astype(jnp.bfloat16), grad_rows, preferred_element_type=jnp.float32
    ).astype(narrow)
    return (query_grad, key_part, value_part)


def per_device(queries, keys, values, cotangent, mask):
    groups = lax.axis_size("y")
    blocks = groups * lax.axis_size("xh") * lax.axis_size("c")
    rows = keys.shape[1]
    tokens = queries.shape[0]
    half = tokens // 2

    flags = mask[:half].astype(jnp.bfloat16)
    served = jnp.stack(
        [
            jnp.concatenate([queries[:half], flags[:, 0].reshape(-1, HD)]),
            jnp.concatenate([cotangent[:half], flags[:, 1].reshape(-1, HD)]),
        ]
    )
    served = passed_along(served, "seq", -1)
    query_next, grad_next = served[0, :half], served[1, :half]
    keep_own_next = served[0, half:].reshape(half).astype(jnp.float32)
    keep_prev_next = served[1, half:].reshape(half).astype(jnp.float32)

    own_kv = jnp.stack([keys[0], values[0]])
    far = lax.axis_size("xh")
    own_kv = jnp.transpose(own_kv, (2, 0, 1, 3)).reshape(KVH, 1, 2, rows * HD)
    own_kv = jnp.broadcast_to(own_kv, (KVH, far, 2, rows * HD)).reshape(-1, 2, rows * HD)
    across = lax.all_to_all(own_kv, ("y", "xh"), split_axis=0, concat_axis=0, tiled=True)
    across = jnp.transpose(across, (1, 0, 2))
    gathered = jnp.concatenate([across, partner(across)], axis=1)
    gathered = jnp.transpose(gathered.reshape(2, blocks, rows, HD), (0, 2, 1, 3))
    gathered = gathered.reshape(2, rows * blocks, HD)
    key_own, value_own = gathered[0], gathered[1]

    keep_own = mask[:, 0]
    keep_prev = mask[:, 1]
    live_rows = (keep_own + keep_prev > 0).astype(jnp.float32)
    score_own, peak_own, total_own, partial_own = block_forward(
        queries, key_own, value_own, keep_own
    )

    score_next = jnp.einsum(
        "rd,kd->rk", query_next, key_own, preferred_element_type=jnp.float32
    ) * HD ** (-0.5)
    peak_next = jnp.max(score_next, axis=1)
    total_next = jnp.sum(jnp.exp(score_next - peak_next[:, None]), axis=1)
    partial_next = jnp.dot(
        jnp.exp(score_next - peak_next[:, None]).astype(jnp.bfloat16),
        value_own,
        preferred_element_type=jnp.float32,
    )
    stats = jnp.concatenate(
        [partial_next, peak_next.reshape(-1, HD), total_next.reshape(-1, HD)]
    )
    stats = passed_along(stats, "seq", 1)
    seen = keep_prev[:half] > 0
    got_peak = stats[half : half + half // HD].reshape(half)
    got_total = stats[half + half // HD :].reshape(half)
    rest = tokens - half
    peak_prev = jnp.concatenate(
        [jnp.where(seen, got_peak, NEGATIVE), jnp.full((rest,), NEGATIVE, jnp.float32)]
    )
    total_prev = jnp.concatenate(
        [jnp.where(seen, got_total, 0.0), jnp.zeros((rest,), jnp.float32)]
    )
    partial_prev = jnp.concatenate(
        [jnp.where(seen[:, None], stats[:half], 0.0), jnp.zeros((rest, HD), jnp.float32)]
    )

    highest = jnp.maximum(peak_own[:half], peak_prev[:half])
    scale_own = jnp.exp(peak_own[:half] - highest)
    scale_prev = jnp.exp(peak_prev[:half] - highest)
    totals = scale_own * total_own[:half] + scale_prev * total_prev[:half]
    attended_head = (
        live_rows[:half, None]
        * (scale_own[:, None] * partial_own[:half] + scale_prev[:, None] * partial_prev[:half])
        / totals[:, None]
    ).astype(jnp.bfloat16)
    delta_head = jnp.sum(
        cotangent[:half].astype(jnp.float32) * attended_head.astype(jnp.float32), axis=1
    )
    attended_tail = (
        live_rows[half:, None] * partial_own[half:] / total_own[half:, None]
    ).astype(jnp.bfloat16)
    delta_tail = jnp.sum(
        cotangent[half:].astype(jnp.float32) * attended_tail.astype(jnp.float32), axis=1
    )
    weights_tail = (
        live_rows[half:, None]
        * jnp.exp(score_own[half:] - peak_own[half:, None])
        / total_own[half:, None]
    )
    gq_tail, gk_tail, gv_tail = finish_backward(
        weights_tail,
        cotangent[half:],
        delta_tail,
        queries[half:],
        key_own,
        value_own,
        jnp.float32,
    )
    attended = jnp.concatenate([attended_head, attended_tail])

    mine = jnp.concatenate(
        [partial_own[:half], peak_own[:half].reshape(-1, HD), total_own[:half].reshape(-1, HD)]
    )
    mine = passed_along(mine, "seq", -1)
    seen_next = keep_prev_next > 0
    live_next = (keep_own_next + keep_prev_next > 0).astype(jnp.float32)
    peak_own_next = mine[half : half + half // HD].reshape(half)
    total_own_next = mine[half + half // HD :].reshape(half)
    peak_prev_next = jnp.where(seen_next, peak_next, NEGATIVE)
    highest_next = jnp.maximum(peak_own_next, peak_prev_next)
    scale_own_next = jnp.exp(peak_own_next - highest_next)
    scale_prev_next = jnp.exp(peak_prev_next - highest_next)
    totals_next = scale_own_next * total_own_next + scale_prev_next * jnp.where(
        seen_next, total_next, 0.0
    )
    totals_next = jnp.where(live_next > 0, totals_next, 1.0)
    attended_next = (
        live_next[:, None]
        * (
            scale_own_next[:, None] * mine[:half]
            + scale_prev_next[:, None] * jnp.where(seen_next[:, None], partial_next, 0.0)
        )
        / totals_next[:, None]
    ).astype(jnp.bfloat16)
    delta_next = jnp.sum(
        grad_next.astype(jnp.float32) * attended_next.astype(jnp.float32), axis=1
    )

    weights_head = (
        live_rows[:half, None] * jnp.exp(score_own[:half] - highest[:, None]) / totals[:, None]
    )
    gq_head, gk_head, gv_head = finish_backward(
        weights_head,
        cotangent[:half],
        delta_head,
        queries[:half],
        key_own,
        value_own,
        jnp.float32,
    )
    gq_own = jnp.concatenate([gq_head, gq_tail])
    gk_own = (gk_head + gk_tail).astype(jnp.bfloat16)
    gv_own = (gv_head + gv_tail).astype(jnp.bfloat16)
    weights_next = jnp.where(
        seen_next[:, None],
        jnp.exp(score_next - highest_next[:, None]) / totals_next[:, None],
        0.0,
    )
    gq_next, gk_next, gv_next = finish_backward(
        weights_next, grad_next, delta_next, query_next, key_own, value_own
    )
    gq_prev = passed_along(gq_next, "seq", 1)
    grad_query = (
        gq_own + jnp.concatenate([gq_prev, jnp.zeros((rest, HD), jnp.float32)])
    ).astype(jnp.bfloat16)

    parts = jnp.stack(
        [
            gk_own.astype(jnp.float32) + gk_next.astype(jnp.float32),
            gv_own.astype(jnp.float32) + gv_next.astype(jnp.float32),
        ]
    ).astype(jnp.bfloat16)
    parts = parts.reshape(2, rows, 2, groups, far, HD)
    summed = parts[:, :, 0].astype(jnp.float32) + partner(parts[:, :, 1]).astype(jnp.float32)
    summed = jnp.transpose(summed.astype(jnp.bfloat16), (2, 3, 0, 1, 4))
    summed = summed.reshape(groups * far, 2, rows, HD)
    summed = lax.all_to_all(summed, ("y", "xh"), split_axis=0, concat_axis=0, tiled=True)
    summed = summed.reshape(KVH, far, 2, rows, HD).astype(jnp.float32).sum(axis=1)
    returned = jnp.transpose(summed, (1, 2, 0, 3)).astype(jnp.bfloat16)
    return (attended, grad_query, returned[0][None], returned[1][None])


def solution(mesh):
    seq_devices, head_devices = mesh.devices.shape
    split = Mesh(
        mesh.devices.reshape(seq_devices, KVH, head_devices // KVH // 2, 2),
        ("seq", "y", "xh", "c"),
    )
    heads = ("y", "xh", "c")
    return jax.shard_map(
        per_device,
        mesh=split,
        in_specs=(
            P("seq", heads),
            P("seq", heads, None, None),
            P("seq", heads, None, None),
            P("seq", heads),
            P("seq", None),
        ),
        out_specs=(
            P("seq", heads),
            P("seq", heads),
            P("seq", heads, None, None),
            P("seq", heads, None, None),
        ),
        check_vma=False,
    )
```

```python
import jax
import jax.numpy as jnp
from jax import lax
from jax.sharding import Mesh
from jax.sharding import PartitionSpec as P

HD = 128
KVH = 8

NEGATIVE = -1e30


def pieces(x):
    hi = x.astype(jnp.bfloat16)
    rest = x - hi.astype(jnp.float32)
    mid = rest.astype(jnp.bfloat16)
    lo = (rest - mid.astype(jnp.float32)).astype(jnp.bfloat16)
    return [hi, mid, lo]


def joined(parts):
    return sum(p.astype(jnp.float32) for p in parts)


def passed_along(value, axis, by):
    length = lax.axis_size(axis)
    pairs = [(i, i + by) for i in range(length) if 0 <= i + by < length]
    return lax.ppermute(value, axis, pairs)


def partner(value):
    return lax.ppermute(value, "c", [(0, 1), (1, 0)])


def block_forward(query_rows, key_rows, value_rows, keep_mask):
    scores = jnp.einsum(
        "rd,kd->rk", query_rows, key_rows, preferred_element_type=jnp.float32
    ) * HD ** (-0.5)
    scores = jnp.where(keep_mask[:, None] > 0, scores, NEGATIVE)
    highest = jnp.max(scores, axis=1)
    powered = jnp.exp(scores - highest[:, None])
    totals = jnp.sum(powered, axis=1)
    partial_value = jnp.dot(
        powered.astype(jnp.bfloat16), value_rows, preferred_element_type=jnp.float32
    )
    return (scores, highest, totals, partial_value)


def finish_backward(
    weights, grad_rows, row_delta, query_rows, key_rows, value_rows, narrow=jnp.bfloat16
):
    grad_weights = jnp.einsum(
        "rd,kd->rk", grad_rows, value_rows, preferred_element_type=jnp.float32
    )
    grad_scores = (weights * (grad_weights - row_delta[:, None]) * HD ** (-0.5)).astype(
        jnp.bfloat16
    )
    query_grad = jnp.dot(grad_scores, key_rows, preferred_element_type=jnp.float32)
    key_part = jnp.einsum(
        "rk,rd->kd", grad_scores, query_rows, preferred_element_type=jnp.float32
    ).astype(narrow)
    value_part = jnp.einsum(
        "rk,rd->kd", weights.astype(jnp.bfloat16), grad_rows, preferred_element_type=jnp.float32
    ).astype(narrow)
    return (query_grad, key_part, value_part)


def per_device(queries, keys, values, cotangent, mask):
    groups = lax.axis_size("y")
    blocks = groups * lax.axis_size("xh") * lax.axis_size("c")
    rows = keys.shape[1]
    tokens = queries.shape[0]
    half = tokens // 2

    flags = mask[:half].astype(jnp.bfloat16)
    served = jnp.stack(
        [
            jnp.concatenate([queries[:half], flags[:, 0].reshape(-1, HD)]),
            jnp.concatenate([cotangent[:half], flags[:, 1].reshape(-1, HD)]),
        ]
    )
    served = passed_along(served, "seq", -1)
    query_next, grad_next = served[0, :half], served[1, :half]
    keep_own_next = served[0, half:].reshape(half).astype(jnp.float32)
    keep_prev_next = served[1, half:].reshape(half).astype(jnp.float32)

    own_kv = jnp.stack([keys[0], values[0]])
    far = lax.axis_size("xh")
    own_kv = jnp.transpose(own_kv, (2, 0, 1, 3)).reshape(KVH, 1, 2, rows * HD)
    own_kv = jnp.broadcast_to(own_kv, (KVH, far, 2, rows * HD)).reshape(-1, 2, rows * HD)
    across = lax.all_to_all(own_kv, ("y", "xh"), split_axis=0, concat_axis=0, tiled=True)
    across = jnp.transpose(across, (1, 0, 2))
    gathered = jnp.concatenate([across, partner(across)], axis=1)
    gathered = jnp.transpose(gathered.reshape(2, blocks, rows, HD), (0, 2, 1, 3))
    gathered = gathered.reshape(2, rows * blocks, HD)
    key_own, value_own = gathered[0], gathered[1]

    keep_own = mask[:, 0]
    keep_prev = mask[:, 1]
    live_rows = (keep_own + keep_prev > 0).astype(jnp.float32)
    score_own, peak_own, total_own, partial_own = block_forward(
        queries, key_own, value_own, keep_own
    )

    score_next = jnp.einsum(
        "rd,kd->rk", query_next, key_own, preferred_element_type=jnp.float32
    ) * HD ** (-0.5)
    peak_next = jnp.max(score_next, axis=1)
    total_next = jnp.sum(jnp.exp(score_next - peak_next[:, None]), axis=1)
    partial_next = jnp.dot(
        jnp.exp(score_next - peak_next[:, None]).astype(jnp.bfloat16),
        value_own,
        preferred_element_type=jnp.float32,
    )
    step = half // HD
    stats = jnp.concatenate(
        [partial_next.astype(jnp.bfloat16)]
        + [p.reshape(-1, HD) for p in pieces(peak_next) + pieces(total_next)]
    )
    stats = passed_along(stats, "seq", 1)
    seen = keep_prev[:half] > 0
    got = [stats[half + i * step : half + (i + 1) * step].reshape(half) for i in range(6)]
    got_peak = joined(got[:3])
    got_total = joined(got[3:])
    rest = tokens - half
    peak_prev = jnp.concatenate(
        [jnp.where(seen, got_peak, NEGATIVE), jnp.full((rest,), NEGATIVE, jnp.float32)]
    )
    total_prev = jnp.concatenate(
        [jnp.where(seen, got_total, 0.0), jnp.zeros((rest,), jnp.float32)]
    )
    partial_prev = jnp.concatenate(
        [
            jnp.where(seen[:, None], stats[:half].astype(jnp.float32), 0.0),
            jnp.zeros((rest, HD), jnp.float32),
        ]
    )

    highest = jnp.maximum(peak_own[:half], peak_prev[:half])
    scale_own = jnp.exp(peak_own[:half] - highest)
    scale_prev = jnp.exp(peak_prev[:half] - highest)
    totals = scale_own * total_own[:half] + scale_prev * total_prev[:half]
    attended_head = (
        live_rows[:half, None]
        * (scale_own[:, None] * partial_own[:half] + scale_prev[:, None] * partial_prev[:half])
        / totals[:, None]
    ).astype(jnp.bfloat16)
    delta_head = jnp.sum(
        cotangent[:half].astype(jnp.float32) * attended_head.astype(jnp.float32), axis=1
    )
    attended_tail = (
        live_rows[half:, None] * partial_own[half:] / total_own[half:, None]
    ).astype(jnp.bfloat16)
    delta_tail = jnp.sum(
        cotangent[half:].astype(jnp.float32) * attended_tail.astype(jnp.float32), axis=1
    )
    weights_tail = (
        live_rows[half:, None]
        * jnp.exp(score_own[half:] - peak_own[half:, None])
        / total_own[half:, None]
    )
    gq_tail, gk_tail, gv_tail = finish_backward(
        weights_tail,
        cotangent[half:],
        delta_tail,
        queries[half:],
        key_own,
        value_own,
        jnp.float32,
    )
    attended = jnp.concatenate([attended_head, attended_tail])

    mine = jnp.concatenate(
        [partial_own[:half].astype(jnp.bfloat16)]
        + [p.reshape(-1, HD) for p in pieces(peak_own[:half]) + pieces(total_own[:half])]
    )
    mine = passed_along(mine, "seq", -1)
    got_next = [mine[half + i * step : half + (i + 1) * step].reshape(half) for i in range(6)]
    seen_next = keep_prev_next > 0
    live_next = (keep_own_next + keep_prev_next > 0).astype(jnp.float32)
    peak_own_next = joined(got_next[:3])
    total_own_next = joined(got_next[3:])
    peak_prev_next = jnp.where(seen_next, peak_next, NEGATIVE)
    highest_next = jnp.maximum(peak_own_next, peak_prev_next)
    scale_own_next = jnp.exp(peak_own_next - highest_next)
    scale_prev_next = jnp.exp(peak_prev_next - highest_next)
    totals_next = scale_own_next * total_own_next + scale_prev_next * jnp.where(
        seen_next, total_next, 0.0
    )
    totals_next = jnp.where(live_next > 0, totals_next, 1.0)
    attended_next = (
        live_next[:, None]
        * (
            scale_own_next[:, None] * mine[:half].astype(jnp.float32)
            + scale_prev_next[:, None] * jnp.where(seen_next[:, None], partial_next, 0.0)
        )
        / totals_next[:, None]
    ).astype(jnp.bfloat16)
    delta_next = jnp.sum(
        grad_next.astype(jnp.float32) * attended_next.astype(jnp.float32), axis=1
    )

    weights_head = (
        live_rows[:half, None] * jnp.exp(score_own[:half] - highest[:, None]) / totals[:, None]
    )
    gq_head, gk_head, gv_head = finish_backward(
        weights_head,
        cotangent[:half],
        delta_head,
        queries[:half],
        key_own,
        value_own,
        jnp.float32,
    )
    gq_own = jnp.concatenate([gq_head, gq_tail])
    gk_own = (gk_head + gk_tail).astype(jnp.bfloat16)
    gv_own = (gv_head + gv_tail).astype(jnp.bfloat16)
    weights_next = jnp.where(
        seen_next[:, None],
        jnp.exp(score_next - highest_next[:, None]) / totals_next[:, None],
        0.0,
    )
    gq_next, gk_next, gv_next = finish_backward(
        weights_next, grad_next, delta_next, query_next, key_own, value_own
    )
    gq_prev = passed_along(gq_next, "seq", 1)
    grad_query = (
        gq_own + jnp.concatenate([gq_prev, jnp.zeros((rest, HD), jnp.float32)])
    ).astype(jnp.bfloat16)

    parts = jnp.stack(
        [
            gk_own.astype(jnp.float32) + gk_next.astype(jnp.float32),
            gv_own.astype(jnp.float32) + gv_next.astype(jnp.float32),
        ]
    ).astype(jnp.bfloat16)
    parts = parts.reshape(2, rows, 2, groups, far, HD)
    summed = parts[:, :, 0].astype(jnp.float32) + partner(parts[:, :, 1]).astype(jnp.float32)
    summed = jnp.transpose(summed.astype(jnp.bfloat16), (2, 3, 0, 1, 4))
    summed = summed.reshape(groups * far, 2, rows, HD)
    summed = lax.all_to_all(summed, ("y", "xh"), split_axis=0, concat_axis=0, tiled=True)
    summed = summed.reshape(KVH, far, 2, rows, HD).astype(jnp.float32).sum(axis=1)
    returned = jnp.transpose(summed, (1, 2, 0, 3)).astype(jnp.bfloat16)
    return (attended, grad_query, returned[0][None], returned[1][None])


def solution(mesh):
    seq_devices, head_devices = mesh.devices.shape
    split = Mesh(
        mesh.devices.reshape(seq_devices, KVH, head_devices // KVH // 2, 2),
        ("seq", "y", "xh", "c"),
    )
    heads = ("y", "xh", "c")
    return jax.shard_map(
        per_device,
        mesh=split,
        in_specs=(
            P("seq", heads),
            P("seq", heads, None, None),
            P("seq", heads, None, None),
            P("seq", heads),
            P("seq", None),
        ),
        out_specs=(
            P("seq", heads),
            P("seq", heads),
            P("seq", heads, None, None),
            P("seq", heads, None, None),
        ),
        check_vma=False,
    )
```

```python
import jax
import jax.numpy as jnp
from jax import lax
from jax.sharding import Mesh
from jax.sharding import PartitionSpec as P

HD = 128
KVH = 8

NEGATIVE = -1e30


def passed_along(value, axis, by):
    length = lax.axis_size(axis)
    pairs = [(i, i + by) for i in range(length) if 0 <= i + by < length]
    return lax.ppermute(value, axis, pairs)


def partner(value):
    return lax.ppermute(value, "c", [(0, 1), (1, 0)])


def block_forward(query_rows, key_rows, value_rows, keep_mask):
    scores = jnp.einsum(
        "rd,kd->rk", query_rows, key_rows, preferred_element_type=jnp.float32
    ) * HD ** (-0.5)
    scores = jnp.where(keep_mask[:, None] > 0, scores, NEGATIVE)
    highest = jnp.max(scores, axis=1)
    powered = jnp.exp(scores - highest[:, None])
    totals = jnp.sum(powered, axis=1)
    partial_value = jnp.dot(
        powered.astype(jnp.bfloat16), value_rows, preferred_element_type=jnp.float32
    )
    return (scores, highest, totals, partial_value)


def finish_backward(
    weights, grad_rows, row_delta, query_rows, key_rows, value_rows, narrow=jnp.bfloat16
):
    grad_weights = jnp.einsum(
        "rd,kd->rk", grad_rows, value_rows, preferred_element_type=jnp.float32
    )
    grad_scores = (weights * (grad_weights - row_delta[:, None]) * HD ** (-0.5)).astype(
        jnp.bfloat16
    )
    query_grad = jnp.dot(grad_scores, key_rows, preferred_element_type=jnp.float32)
    key_part = jnp.einsum(
        "rk,rd->kd", grad_scores, query_rows, preferred_element_type=jnp.float32
    ).astype(narrow)
    value_part = jnp.einsum(
        "rk,rd->kd", weights.astype(jnp.bfloat16), grad_rows, preferred_element_type=jnp.float32
    ).astype(narrow)
    return (query_grad, key_part, value_part)


def per_device(queries, keys, values, cotangent, mask):
    groups = lax.axis_size("y")
    blocks = groups * lax.axis_size("xh") * lax.axis_size("c")
    rows = keys.shape[1]
    tokens = queries.shape[0]
    half = tokens // 2

    flags = mask[:half].astype(jnp.bfloat16)
    served = jnp.stack(
        [
            jnp.concatenate([queries[:half], flags[:, 0].reshape(-1, HD)]),
            jnp.concatenate([cotangent[:half], flags[:, 1].reshape(-1, HD)]),
        ]
    )
    served = passed_along(served, "seq", -1)
    query_next, grad_next = served[0, :half], served[1, :half]
    keep_own_next = served[0, half:].reshape(half).astype(jnp.float32)
    keep_prev_next = served[1, half:].reshape(half).astype(jnp.float32)

    own_kv = jnp.stack([keys[0], values[0]])
    far = lax.axis_size("xh")
    own_kv = jnp.transpose(own_kv, (2, 0, 1, 3)).reshape(KVH, 1, 2, rows * HD)
    own_kv = jnp.broadcast_to(own_kv, (KVH, far, 2, rows * HD)).reshape(-1, 2, rows * HD)
    across = lax.all_to_all(own_kv, ("y", "xh"), split_axis=0, concat_axis=0, tiled=True)
    across = jnp.transpose(across, (1, 0, 2))
    gathered = jnp.concatenate([across, partner(across)], axis=1)
    gathered = jnp.transpose(gathered.reshape(2, blocks, rows, HD), (0, 2, 1, 3))
    gathered = gathered.reshape(2, rows * blocks, HD)
    key_own, value_own = gathered[0], gathered[1]

    keep_own = mask[:, 0]
    keep_prev = mask[:, 1]
    live_rows = (keep_own + keep_prev > 0).astype(jnp.float32)
    own = [
        block_forward(queries[:half], key_own, value_own, keep_own[:half]),
        block_forward(queries[half:], key_own, value_own, keep_own[half:]),
    ]
    score_own, peak_own, total_own, partial_own = (
        jnp.concatenate([own[0][i], own[1][i]]) for i in range(4)
    )

    score_next = jnp.einsum(
        "rd,kd->rk", query_next, key_own, preferred_element_type=jnp.float32
    ) * HD ** (-0.5)
    peak_next = jnp.max(score_next, axis=1)
    total_next = jnp.sum(jnp.exp(score_next - peak_next[:, None]), axis=1)
    partial_next = jnp.dot(
        jnp.exp(score_next - peak_next[:, None]).astype(jnp.bfloat16),
        value_own,
        preferred_element_type=jnp.float32,
    )
    stats = jnp.concatenate(
        [partial_next, peak_next.reshape(-1, HD), total_next.reshape(-1, HD)]
    )
    stats = passed_along(stats, "seq", 1)
    seen = keep_prev[:half] > 0
    got_peak = stats[half : half + half // HD].reshape(half)
    got_total = stats[half + half // HD :].reshape(half)
    rest = tokens - half
    peak_prev = jnp.concatenate(
        [jnp.where(seen, got_peak, NEGATIVE), jnp.full((rest,), NEGATIVE, jnp.float32)]
    )
    total_prev = jnp.concatenate(
        [jnp.where(seen, got_total, 0.0), jnp.zeros((rest,), jnp.float32)]
    )
    partial_prev = jnp.concatenate(
        [jnp.where(seen[:, None], stats[:half], 0.0), jnp.zeros((rest, HD), jnp.float32)]
    )

    highest = jnp.maximum(peak_own[:half], peak_prev[:half])
    scale_own = jnp.exp(peak_own[:half] - highest)
    scale_prev = jnp.exp(peak_prev[:half] - highest)
    totals = scale_own * total_own[:half] + scale_prev * total_prev[:half]
    attended_head = (
        live_rows[:half, None]
        * (scale_own[:, None] * partial_own[:half] + scale_prev[:, None] * partial_prev[:half])
        / totals[:, None]
    ).astype(jnp.bfloat16)
    delta_head = jnp.sum(
        cotangent[:half].astype(jnp.float32) * attended_head.astype(jnp.float32), axis=1
    )
    attended_tail = (
        live_rows[half:, None] * partial_own[half:] / total_own[half:, None]
    ).astype(jnp.bfloat16)
    delta_tail = jnp.sum(
        cotangent[half:].astype(jnp.float32) * attended_tail.astype(jnp.float32), axis=1
    )
    weights_tail = (
        live_rows[half:, None]
        * jnp.exp(score_own[half:] - peak_own[half:, None])
        / total_own[half:, None]
    )
    gq_tail, gk_tail, gv_tail = finish_backward(
        weights_tail,
        cotangent[half:],
        delta_tail,
        queries[half:],
        key_own,
        value_own,
        jnp.float32,
    )
    attended = jnp.concatenate([attended_head, attended_tail])

    mine = jnp.concatenate(
        [partial_own[:half], peak_own[:half].reshape(-1, HD), total_own[:half].reshape(-1, HD)]
    )
    mine = passed_along(mine, "seq", -1)
    seen_next = keep_prev_next > 0
    live_next = (keep_own_next + keep_prev_next > 0).astype(jnp.float32)
    peak_own_next = mine[half : half + half // HD].reshape(half)
    total_own_next = mine[half + half // HD :].reshape(half)
    peak_prev_next = jnp.where(seen_next, peak_next, NEGATIVE)
    highest_next = jnp.maximum(peak_own_next, peak_prev_next)
    scale_own_next = jnp.exp(peak_own_next - highest_next)
    scale_prev_next = jnp.exp(peak_prev_next - highest_next)
    totals_next = scale_own_next * total_own_next + scale_prev_next * jnp.where(
        seen_next, total_next, 0.0
    )
    totals_next = jnp.where(live_next > 0, totals_next, 1.0)
    attended_next = (
        live_next[:, None]
        * (
            scale_own_next[:, None] * mine[:half]
            + scale_prev_next[:, None] * jnp.where(seen_next[:, None], partial_next, 0.0)
        )
        / totals_next[:, None]
    ).astype(jnp.bfloat16)
    delta_next = jnp.sum(
        grad_next.astype(jnp.float32) * attended_next.astype(jnp.float32), axis=1
    )

    weights_head = (
        live_rows[:half, None] * jnp.exp(score_own[:half] - highest[:, None]) / totals[:, None]
    )
    gq_head, gk_head, gv_head = finish_backward(
        weights_head,
        cotangent[:half],
        delta_head,
        queries[:half],
        key_own,
        value_own,
        jnp.float32,
    )
    gq_own = jnp.concatenate([gq_head, gq_tail])
    gk_own = (gk_head + gk_tail).astype(jnp.bfloat16)
    gv_own = (gv_head + gv_tail).astype(jnp.bfloat16)
    weights_next = jnp.where(
        seen_next[:, None],
        jnp.exp(score_next - highest_next[:, None]) / totals_next[:, None],
        0.0,
    )
    gq_next, gk_next, gv_next = finish_backward(
        weights_next, grad_next, delta_next, query_next, key_own, value_own
    )
    gq_prev = passed_along(gq_next, "seq", 1)
    grad_query = (
        gq_own + jnp.concatenate([gq_prev, jnp.zeros((rest, HD), jnp.float32)])
    ).astype(jnp.bfloat16)

    parts = jnp.stack(
        [
            gk_own.astype(jnp.float32) + gk_next.astype(jnp.float32),
            gv_own.astype(jnp.float32) + gv_next.astype(jnp.float32),
        ]
    ).astype(jnp.bfloat16)
    parts = parts.reshape(2, rows, 2, groups, far, HD)
    summed = parts[:, :, 0].astype(jnp.float32) + partner(parts[:, :, 1]).astype(jnp.float32)
    summed = jnp.transpose(summed.astype(jnp.bfloat16), (2, 3, 0, 1, 4))
    summed = summed.reshape(groups * far, 2, rows, HD)
    summed = lax.all_to_all(summed, ("y", "xh"), split_axis=0, concat_axis=0, tiled=True)
    summed = summed.reshape(KVH, far, 2, rows, HD).astype(jnp.float32).sum(axis=1)
    returned = jnp.transpose(summed, (1, 2, 0, 3)).astype(jnp.bfloat16)
    return (attended, grad_query, returned[0][None], returned[1][None])


def solution(mesh):
    seq_devices, head_devices = mesh.devices.shape
    split = Mesh(
        mesh.devices.reshape(seq_devices, KVH, head_devices // KVH // 2, 2),
        ("seq", "y", "xh", "c"),
    )
    heads = ("y", "xh", "c")
    return jax.shard_map(
        per_device,
        mesh=split,
        in_specs=(
            P("seq", heads),
            P("seq", heads, None, None),
            P("seq", heads, None, None),
            P("seq", heads),
            P("seq", None),
        ),
        out_specs=(
            P("seq", heads),
            P("seq", heads),
            P("seq", heads, None, None),
            P("seq", heads, None, None),
        ),
        check_vma=False,
    )
```

```python
import jax
import jax.numpy as jnp
from jax import lax
from jax.sharding import Mesh
from jax.sharding import PartitionSpec as P

HD = 128
KVH = 8

NEGATIVE = -1e30


def passed_along(value, axis, by):
    length = lax.axis_size(axis)
    pairs = [(i, i + by) for i in range(length) if 0 <= i + by < length]
    return lax.ppermute(value, axis, pairs)


def partner(value):
    return lax.ppermute(value, "c", [(0, 1), (1, 0)])


def block_forward(query_rows, key_rows, value_rows, keep_mask):
    scores = jnp.einsum(
        "rd,kd->rk", query_rows, key_rows, preferred_element_type=jnp.float32
    ) * HD ** (-0.5)
    scores = jnp.where(keep_mask[:, None] > 0, scores, NEGATIVE)
    highest = jnp.max(scores, axis=1)
    powered = jnp.exp(scores - highest[:, None])
    totals = jnp.sum(powered, axis=1)
    partial_value = jnp.dot(
        powered.astype(jnp.bfloat16), value_rows, preferred_element_type=jnp.float32
    )
    return (scores, highest, totals, partial_value)


def finish_backward(
    weights, grad_rows, row_delta, query_rows, key_rows, value_rows, narrow=jnp.bfloat16
):
    grad_weights = jnp.einsum(
        "rd,kd->rk", grad_rows, value_rows, preferred_element_type=jnp.float32
    )
    grad_scores = (weights * (grad_weights - row_delta[:, None]) * HD ** (-0.5)).astype(
        jnp.bfloat16
    )
    query_grad = jnp.dot(grad_scores, key_rows, preferred_element_type=jnp.float32)
    key_part = jnp.einsum(
        "rk,rd->kd", grad_scores, query_rows, preferred_element_type=jnp.float32
    ).astype(narrow)
    value_part = jnp.einsum(
        "rk,rd->kd", weights.astype(jnp.bfloat16), grad_rows, preferred_element_type=jnp.float32
    ).astype(narrow)
    return (query_grad, key_part, value_part)


def per_device(queries, keys, values, cotangent, mask):
    groups = lax.axis_size("y")
    blocks = groups * lax.axis_size("xh") * lax.axis_size("c")
    rows = keys.shape[1]
    tokens = queries.shape[0]
    half = tokens // 2

    flags = mask[:half].astype(jnp.bfloat16)
    served = jnp.stack(
        [
            jnp.concatenate([queries[:half], flags[:, 0].reshape(-1, HD)]),
            jnp.concatenate([cotangent[:half], flags[:, 1].reshape(-1, HD)]),
        ]
    )
    served = passed_along(served, "seq", -1)
    query_next, grad_next = served[0, :half], served[1, :half]
    keep_own_next = served[0, half:].reshape(half).astype(jnp.float32)
    keep_prev_next = served[1, half:].reshape(half).astype(jnp.float32)

    own_kv = jnp.stack([keys[0], values[0]])
    far = lax.axis_size("xh")
    own_kv = jnp.transpose(own_kv, (2, 0, 1, 3)).reshape(KVH, 1, 2, rows * HD)
    own_kv = jnp.broadcast_to(own_kv, (KVH, far, 2, rows * HD)).reshape(-1, 2, rows * HD)
    across = lax.all_to_all(own_kv, ("y", "xh"), split_axis=0, concat_axis=0, tiled=True)
    across = jnp.transpose(across, (1, 0, 2))
    gathered = jnp.concatenate([across, partner(across)], axis=1)
    gathered = jnp.transpose(gathered.reshape(2, blocks, rows, HD), (0, 2, 1, 3))
    gathered = gathered.reshape(2, rows * blocks, HD)
    key_own, value_own = gathered[0], gathered[1]

    keep_own = mask[:, 0]
    keep_prev = mask[:, 1]
    live_rows = (keep_own + keep_prev > 0).astype(jnp.float32)
    score_own, peak_own, total_own, partial_own = block_forward(
        queries, key_own, value_own, keep_own
    )

    score_next = jnp.einsum(
        "rd,kd->rk", query_next, key_own, preferred_element_type=jnp.float32
    ) * HD ** (-0.5)
    peak_next = jnp.max(score_next, axis=1)
    total_next = jnp.sum(jnp.exp(score_next - peak_next[:, None]), axis=1)
    partial_next = jnp.dot(
        jnp.exp(score_next - peak_next[:, None]).astype(jnp.bfloat16),
        value_own,
        preferred_element_type=jnp.float32,
    )
    stats = jnp.concatenate(
        [partial_next, peak_next.reshape(-1, HD), total_next.reshape(-1, HD)]
    )
    stats = passed_along(stats, "seq", 1)
    seen = keep_prev[:half] > 0
    got_peak = stats[half : half + half // HD].reshape(half)
    got_total = stats[half + half // HD :].reshape(half)
    rest = tokens - half
    peak_prev = jnp.concatenate(
        [jnp.where(seen, got_peak, NEGATIVE), jnp.full((rest,), NEGATIVE, jnp.float32)]
    )
    total_prev = jnp.concatenate(
        [jnp.where(seen, got_total, 0.0), jnp.zeros((rest,), jnp.float32)]
    )
    partial_prev = jnp.concatenate(
        [jnp.where(seen[:, None], stats[:half], 0.0), jnp.zeros((rest, HD), jnp.float32)]
    )

    highest = jnp.maximum(peak_own[:half], peak_prev[:half])
    scale_own = jnp.exp(peak_own[:half] - highest)
    scale_prev = jnp.exp(peak_prev[:half] - highest)
    totals = scale_own * total_own[:half] + scale_prev * total_prev[:half]
    attended_head = (
        live_rows[:half, None]
        * (scale_own[:, None] * partial_own[:half] + scale_prev[:, None] * partial_prev[:half])
        / totals[:, None]
    ).astype(jnp.bfloat16)
    delta_head = jnp.sum(
        cotangent[:half].astype(jnp.float32) * attended_head.astype(jnp.float32), axis=1
    )
    attended_tail = (
        live_rows[half:, None] * partial_own[half:] / total_own[half:, None]
    ).astype(jnp.bfloat16)
    delta_tail = jnp.sum(
        cotangent[half:].astype(jnp.float32) * attended_tail.astype(jnp.float32), axis=1
    )
    weights_tail = (
        live_rows[half:, None]
        * jnp.exp(score_own[half:] - peak_own[half:, None])
        / total_own[half:, None]
    )
    gq_tail, gk_tail, gv_tail = finish_backward(
        weights_tail,
        cotangent[half:],
        delta_tail,
        queries[half:],
        key_own,
        value_own,
        jnp.float32,
    )
    attended = jnp.concatenate([attended_head, attended_tail])

    mine = jnp.concatenate(
        [partial_own[:half], peak_own[:half].reshape(-1, HD), total_own[:half].reshape(-1, HD)]
    )
    mine = passed_along(mine, "seq", -1)
    seen_next = keep_prev_next > 0
    live_next = (keep_own_next + keep_prev_next > 0).astype(jnp.float32)
    peak_own_next = mine[half : half + half // HD].reshape(half)
    total_own_next = mine[half + half // HD :].reshape(half)
    peak_prev_next = jnp.where(seen_next, peak_next, NEGATIVE)
    highest_next = jnp.maximum(peak_own_next, peak_prev_next)
    scale_own_next = jnp.exp(peak_own_next - highest_next)
    scale_prev_next = jnp.exp(peak_prev_next - highest_next)
    totals_next = scale_own_next * total_own_next + scale_prev_next * jnp.where(
        seen_next, total_next, 0.0
    )
    totals_next = jnp.where(live_next > 0, totals_next, 1.0)
    attended_next = (
        live_next[:, None]
        * (
            scale_own_next[:, None] * mine[:half]
            + scale_prev_next[:, None] * jnp.where(seen_next[:, None], partial_next, 0.0)
        )
        / totals_next[:, None]
    ).astype(jnp.bfloat16)
    delta_next = jnp.sum(
        grad_next.astype(jnp.float32) * attended_next.astype(jnp.float32), axis=1
    )

    weights_head = (
        live_rows[:half, None] * jnp.exp(score_own[:half] - highest[:, None]) / totals[:, None]
    )
    gq_head, gk_head, gv_head = finish_backward(
        weights_head,
        cotangent[:half],
        delta_head,
        queries[:half],
        key_own,
        value_own,
        jnp.float32,
    )
    gq_own = jnp.concatenate([gq_head, gq_tail])
    gk_own = (gk_head + gk_tail).astype(jnp.bfloat16)
    gv_own = (gv_head + gv_tail).astype(jnp.bfloat16)
    weights_next = jnp.where(
        seen_next[:, None],
        jnp.exp(score_next - highest_next[:, None]) / totals_next[:, None],
        0.0,
    )
    gq_next, gk_next, gv_next = finish_backward(
        weights_next, grad_next, delta_next, query_next, key_own, value_own
    )
    gq_prev = passed_along(gq_next.astype(jnp.bfloat16), "seq", 1).astype(jnp.float32)
    grad_query = (
        gq_own + jnp.concatenate([gq_prev, jnp.zeros((rest, HD), jnp.float32)])
    ).astype(jnp.bfloat16)

    parts = jnp.stack(
        [
            gk_own.astype(jnp.float32) + gk_next.astype(jnp.float32),
            gv_own.astype(jnp.float32) + gv_next.astype(jnp.float32),
        ]
    ).astype(jnp.bfloat16)
    parts = parts.reshape(2, rows, 2, groups, far, HD)
    summed = parts[:, :, 0].astype(jnp.float32) + partner(parts[:, :, 1]).astype(jnp.float32)
    summed = jnp.transpose(summed.astype(jnp.bfloat16), (2, 3, 0, 1, 4))
    summed = summed.reshape(groups * far, 2, rows, HD)
    summed = lax.all_to_all(summed, ("y", "xh"), split_axis=0, concat_axis=0, tiled=True)
    summed = summed.reshape(KVH, far, 2, rows, HD).astype(jnp.float32).sum(axis=1)
    returned = jnp.transpose(summed, (1, 2, 0, 3)).astype(jnp.bfloat16)
    return (attended, grad_query, returned[0][None], returned[1][None])


def solution(mesh):
    seq_devices, head_devices = mesh.devices.shape
    split = Mesh(
        mesh.devices.reshape(seq_devices, KVH, head_devices // KVH // 2, 2),
        ("seq", "y", "xh", "c"),
    )
    heads = ("y", "xh", "c")
    return jax.shard_map(
        per_device,
        mesh=split,
        in_specs=(
            P("seq", heads),
            P("seq", heads, None, None),
            P("seq", heads, None, None),
            P("seq", heads),
            P("seq", None),
        ),
        out_specs=(
            P("seq", heads),
            P("seq", heads),
            P("seq", heads, None, None),
            P("seq", heads, None, None),
        ),
        check_vma=False,
    )
```
